32 devices in a mesh: grp: 4 (over y, x), rows: 8 (over z, core).
Axes of the slice: x: 2, y: 2, z: 4, core: 2. Of those that a mesh axis runs over, the one named last changes fastest.
Arguments:
- stationary: bfloat16 [81920, 512], P(('grp', 'rows')), may hold values from -6 to 6
- rotor_rows: bfloat16 [1024, 512], P(('grp', 'rows')), may hold values from -6 to 6
- owners: int32 [1024, 1], P(('grp', 'rows')), may hold values from 0 to 7; in each aligned block of 32 rows (0 to 31, 32 to 63, ...) at most 6 rows name the same one
- counts: int32 [32], P(('grp', 'rows')), may hold values from 24 to 32
- omega: bfloat16 [512, 192], replicated, may hold values from -0.25 to 0.25
Outputs:
- basis_stationary: bfloat16 [81920, 192], P(('grp', 'rows'))
- basis_rotor: bfloat16 [1536, 192], P(('grp', 'rows'))
- factor: float32 [192, 192], replicated
The draws below stay inside these ranges and needn't reach their ends.
Inputs may be any that keep to these rules, and one draw needn't show every extreme that they name: `owners`: in the rotor rows of one device no owner is named more than 6 times.
All inputs are finite; a program needn't handle non-finite values.
Results may differ from the reference program's by a relative error of at most 0.0056.
Values may be sent and summed in bfloat16 or wider, within the bound.
No kernel may reach another device: no remote copies, remote signals or barrier semaphores. Data moves between devices by JAX's collectives and lax.ppermute only.
A program may use at most 64 MiB of HBM per device.

```python
import math
import jax
import jax.numpy as jnp
import numpy as np
from jax import lax

W = 512
K = 192
STAT_DEV = 2560
CAP = 6
ROT_DEV = 32
STAT_TOTAL = 81920
ROTOR_TOTAL = 1024
SLOTS = 1536
N_GRP = 4
N_ROWS = 8


def draw_counts(key, part):
    keys = jax.random.split(jax.random.fold_in(key, 17), 3)
    lowest = 3 * ROT_DEV // 4
    devices = N_GRP * N_ROWS
    values = jax.random.randint(keys[0], (devices,), lowest, ROT_DEV + 1)
    first = jax.random.randint(keys[1], (), 0, devices)
    values = values.at[first].set(ROT_DEV)
    second = (first + 1 + jax.random.randint(keys[2], (), 0, devices - 1)) % devices
    values = values.at[second].set(lowest)
    return values.astype(jnp.int32)


def level_of(stream_key, dims, cuts, low, largest):
    gain, own = 1.0, jax.random.fold_in(stream_key, 6)
    for position, shards_of in cuts:
        steps = jnp.exp(jax.random.uniform(jax.random.fold_in(own, position), (shards_of,), jnp.float32, low / len(cuts), largest / len(cuts)))
        gain = gain * jnp.repeat(steps, dims[position] // shards_of).reshape([-1 if axis == position else 1 for axis in range(len(dims))])
    return gain


def assign_block(key, own, number, rows, amount, top, bound, slope):
    ranking = jax.random.permutation(key, amount)
    packed, ordinary = shares(amount, rows * top, bound, slope, True), shares(amount, rows * top, bound, slope, False)
    places = jnp.arange(amount)

    def named(lengths, turn):
        used = int((lengths > 0).sum())
        fixed = max(1, used // 4)
        moved = fixed + (places - fixed + turn * (used - fixed)) % max(1, amount - fixed)
        return jnp.zeros((amount,), jnp.int32).at[ranking[jnp.where(places < fixed, places, moved)]].set(jnp.asarray(lengths, jnp.int32))

    lengths = jnp.where(number % 4 == 0, named(packed, number // 4), named(ordinary, number - number // 4 - 1))
    mixed = jax.random.permutation(jax.random.fold_in(own, 3), amount)
    donor, receiver = mixed[0:amount // 2 * 2:2], mixed[1:amount // 2 * 2:2]
    slack = jnp.minimum(lengths[donor] - 1, bound - lengths[receiver]) // 2
    slack = jnp.where((donor == ranking[0]) | (receiver == ranking[0]) | (lengths[receiver] == 0), 0, jnp.maximum(slack, 0))
    moved = jax.random.randint(jax.random.fold_in(own, 4), (amount // 2,), 0, 1 << 20) % (slack + 1)
    lengths = lengths.at[donor].add(-moved).at[receiver].add(moved)
    items = jnp.searchsorted(jnp.cumsum(lengths), jnp.arange(rows * top), side="right").astype(jnp.int32)
    listing = items.reshape(top, rows).T
    listing = listing[jax.random.permutation(jax.random.fold_in(own, 1), rows)]
    turn = jax.random.randint(jax.random.fold_in(own, 2), (rows, 1), 0, top)
    return jnp.take_along_axis(listing, (jnp.arange(top)[None, :] + turn) % top, axis=1)


def shares(number_of, total, bound, skew, full):
    weights = [(1 << 20) // math.isqrt(grade ** skew) + 1 for grade in range(1, number_of + 1)]
    largest = bound if full else min(bound, max(-(-total // number_of), total * weights[0] // sum(weights)))
    least = 1 if total - largest >= number_of - 1 else 0
    holding, spare = [largest] + [least] * (number_of - 1), total - largest - least * (number_of - 1)
    while spare > 0:
        free = [i for i in range(1, number_of) if holding[i] < largest] or [i for i in range(1, number_of) if holding[i] < bound]
        mass, budget = sum([weights[i] for i in free]), spare
        for i in free:
            addition = min(bound - holding[i], max(1, budget * weights[i] // mass), spare)
            holding[i] = holding[i] + addition
            spare = spare - addition
    return np.array(holding)


def noise(key, dims, spread, limit, cuts=(), held_as=jnp.bfloat16):
    drawn = spread * jax.random.normal(key, dims, jnp.float32)
    if cuts:
        drawn = drawn * level_of(key, dims, cuts, -0.22, 0.18)
    return jnp.clip(drawn, -limit, limit).astype(held_as)


def setup_inputs(seed: int = 0) -> dict:
    key_list = jax.random.split(jax.random.key(seed), 6)
    stationary = noise(key_list[0], (STAT_TOTAL, W), 1.0, 6.0, ((0, 32),))
    rotor_rows = noise(key_list[1], (ROTOR_TOTAL, W), 1.0, 6.0, ((0, 32),))
    owners_keys = jax.random.split(jax.random.fold_in(key_list[2], 1), ROTOR_TOTAL // ROT_DEV)
    owners_turns = jax.random.permutation(jax.random.fold_in(key_list[2], 3), ROTOR_TOTAL // ROT_DEV)
    owners = jax.vmap(lambda own, number: assign_block(jax.random.fold_in(key_list[2], 2), own, number, ROT_DEV, N_ROWS, 1, CAP, 2))(owners_keys, owners_turns).reshape((ROTOR_TOTAL, 1))
    counts = draw_counts(jax.random.fold_in(key_list[5], 71), 0)
    omega = noise(key_list[4], (W, K), W ** -0.5, 0.25)
    return {"stationary": stationary, "rotor_rows": rotor_rows, "owners": owners, "counts": counts, "omega": omega}


def sketch_block(block, omega):
    return jnp.dot(block.astype(jnp.float32), omega.astype(jnp.float32), preferred_element_type=jnp.float32).astype(jnp.bfloat16)

def reference(stationary, rotor_rows, owners, counts, omega):
    devices = N_GRP * N_ROWS
    total = (STAT_DEV + ROT_DEV) * devices
    stat_blocks = stationary.reshape(devices, STAT_DEV, W)
    rotor_sketch = sketch_block(rotor_rows, omega).reshape(N_GRP, N_ROWS, ROT_DEV, K)
    targets = owners[:, 0].reshape(N_GRP, N_ROWS, ROT_DEV)
    positions = lax.broadcasted_iota(jnp.int32, (N_GRP, N_ROWS, ROT_DEV), 2)
    live = positions < counts.reshape(N_GRP, N_ROWS)[:, :, None]
    onehot = ((targets[..., None] == jnp.arange(N_ROWS, dtype=jnp.int32)) & live[..., None]).astype(jnp.int32)
    rank = jnp.sum((jnp.cumsum(onehot, axis=2) - onehot) * onehot, axis=3)
    slot = jnp.where(live, rank, CAP).astype(jnp.int32)
    group_idx = lax.broadcasted_iota(jnp.int32, (N_GRP, N_ROWS, ROT_DEV), 0)
    sender_idx = lax.broadcasted_iota(jnp.int32, (N_GRP, N_ROWS, ROT_DEV), 1)
    placed = jnp.zeros((N_GRP, N_ROWS, N_ROWS, CAP + 1, K), rotor_sketch.dtype)
    placed = placed.at[group_idx, targets, sender_idx, slot].set(rotor_sketch)
    rotor_local = placed[:, :, :, :CAP, :].reshape(devices, N_ROWS * CAP, K)

    def local_rows(block, rotor_part):
        return jnp.concatenate([sketch_block(block, omega), rotor_part], axis=0)

    def accumulate(gram, items):
        ymat = local_rows(items[0], items[1])
        term = lax.dot_general(ymat.astype(jnp.float32), ymat.astype(jnp.float32), (((0,), (0,)), ((), ())), preferred_element_type=jnp.float32)
        return (gram + term / total, None)
    gram, _ = lax.scan(accumulate, jnp.zeros((K, K), jnp.float32), (stat_blocks, rotor_local))
    lower = jnp.linalg.cholesky(gram)

    def solve_block(items):
        ymat = local_rows(items[0], items[1]).astype(jnp.float32)
        sol = lax.linalg.triangular_solve(lower, ymat.T, left_side=True, lower=True)
        basis = sol.T.astype(jnp.bfloat16)
        return (basis[:STAT_DEV], basis[STAT_DEV:])
    basis_stat, basis_rot = lax.map(solve_block, (stat_blocks, rotor_local))
    return (basis_stat.reshape(STAT_TOTAL, K), basis_rot.reshape(SLOTS, K), lower.T)
```

```python
import jax
import jax.numpy as jnp
from jax import lax
from jax.sharding import PartitionSpec as P

CAP = 6
AXES = ("grp", "rows")


def sketch_block(block, omega):
    return jnp.dot(block, omega, preferred_element_type=jnp.float32).astype(jnp.bfloat16)


def pack_sym(g):
    h = g.shape[0] // 2
    i = lax.broadcasted_iota(jnp.int32, (h, h), 0)
    j = lax.broadcasted_iota(jnp.int32, (h, h), 1)
    a, b, c = g[:h, :h], g[h:, :h], g[h:, h:]
    m = jnp.where(i >= j, a, c)
    diag_c = jnp.sum(jnp.where(i == j, c, 0.0), axis=0, keepdims=True)
    return jnp.concatenate([b, m, diag_c], axis=0)


def unpack_sym(p):
    h = p.shape[1]
    b, m, diag_c = p[:h], p[h : 2 * h], p[2 * h :]
    i = lax.broadcasted_iota(jnp.int32, (h, h), 0)
    j = lax.broadcasted_iota(jnp.int32, (h, h), 1)
    mt = m.T
    a = jnp.where(i >= j, m, mt)
    c = jnp.where(i < j, m, jnp.where(i > j, mt, diag_c))
    return jnp.concatenate(
        [jnp.concatenate([a, b.T], axis=1), jnp.concatenate([b, c], axis=1)], axis=0
    )


def all_sum(x, n):
    if n & (n - 1):
        return lax.psum(x, AXES)
    bits = n.bit_length() - 1
    for b in reversed(range(bits)):
        x = x + lax.ppermute(x, AXES, [(i, i ^ (1 << b)) for i in range(n)])
    return x


def per_device(stationary, rotor_rows, owners, counts, omega):
    n_rows = lax.axis_size("rows")
    n_grp = lax.axis_size("grp")
    rot_dev = rotor_rows.shape[0]
    stat_dev = stationary.shape[0]
    total = n_grp * n_rows * (stat_dev + rot_dev)
    targets = owners[:, 0]
    live = lax.iota(jnp.int32, rot_dev) < counts[0]
    onehot = ((targets[:, None] == lax.iota(jnp.int32, n_rows)[None, :]) & live[:, None]).astype(
        jnp.int32
    )
    rank = jnp.sum((jnp.cumsum(onehot, axis=0) - onehot) * onehot, axis=1)
    slot = jnp.where(live, targets * CAP + rank, -1)
    select = (lax.iota(jnp.int32, n_rows * CAP)[:, None] == slot[None, :]).astype(jnp.bfloat16)

    sketch_stat = sketch_block(stationary, omega)
    sketch_rot = sketch_block(rotor_rows, omega)
    rot_live = jnp.where(live[:, None], sketch_rot, jnp.zeros_like(sketch_rot))

    dims = (((0,), (0,)), ((), ()))
    gram = lax.dot_general(sketch_stat, sketch_stat, dims, preferred_element_type=jnp.float32)
    gram = gram + lax.dot_general(rot_live, rot_live, dims, preferred_element_type=jnp.float32)
    gram = gram / total

    outgoing = jnp.dot(select, sketch_rot, preferred_element_type=jnp.float32).astype(jnp.bfloat16)
    outgoing = outgoing.reshape(n_rows, CAP, -1)
    arrived = lax.all_to_all(outgoing, "rows", split_axis=0, concat_axis=0, tiled=True)
    arrived = arrived.reshape(n_rows * CAP, -1)

    gram = unpack_sym(all_sum(pack_sym(gram), n_grp * n_rows))
    lower = jnp.linalg.cholesky(gram)
    local = jnp.concatenate([sketch_stat, arrived], axis=0)
    solved = lax.linalg.triangular_solve(
        lower, local.astype(jnp.float32).T, left_side=True, lower=True
    )
    basis = solved.T.astype(jnp.bfloat16)
    return (basis[:stat_dev], basis[stat_dev:], lower.T)


def solution(mesh):
    return jax.shard_map(
        per_device,
        mesh=mesh,
        in_specs=(
            P(("grp", "rows"), None),
            P(("grp", "rows"), None),
            P(("grp", "rows"), None),
            P(("grp", "rows")),
            P(),
        ),
        out_specs=(P(("grp", "rows"), None), P(("grp", "rows"), None), P()),
        check_vma=False,
    )
```

```python
import jax
import jax.numpy as jnp
from jax import lax
from jax.sharding import PartitionSpec as P

CAP = 6
AXES = ("grp", "rows")
HIGHEST = lax.Precision.HIGHEST


def sketch_block(block, omega):
    return jnp.dot(block, omega, preferred_element_type=jnp.float32).astype(jnp.bfloat16)


def pack_sym(g):
    h = g.shape[0] // 2
    i = lax.broadcasted_iota(jnp.int32, (h, h), 0)
    j = lax.broadcasted_iota(jnp.int32, (h, h), 1)
    a, b, c = g[:h, :h], g[h:, :h], g[h:, h:]
    m = jnp.where(i >= j, a, c)
    diag_c = jnp.sum(jnp.where(i == j, c, 0.0), axis=0, keepdims=True)
    return jnp.concatenate([b, m, diag_c], axis=0)


def unpack_sym(p):
    h = p.shape[1]
    b, m, diag_c = p[:h], p[h : 2 * h], p[2 * h :]
    i = lax.broadcasted_iota(jnp.int32, (h, h), 0)
    j = lax.broadcasted_iota(jnp.int32, (h, h), 1)
    mt = m.T
    a = jnp.where(i >= j, m, mt)
    c = jnp.where(i < j, m, jnp.where(i > j, mt, diag_c))
    return jnp.concatenate(
        [jnp.concatenate([a, b.T], axis=1), jnp.concatenate([b, c], axis=1)], axis=0
    )


def all_sum(x, n):
    if n & (n - 1):
        return lax.psum(x, AXES)
    bits = n.bit_length() - 1
    for b in reversed(range(bits)):
        x = x + lax.ppermute(x, AXES, [(i, i ^ (1 << b)) for i in range(n)])
    return x


def cholesky_and_inverse(g):
    k = g.shape[0]
    h = k // 2
    a11, a21, a22 = g[:h, :h], g[h:, :h], g[h:, h:]
    eye = jnp.eye(h, dtype=jnp.float32)
    l11 = lax.linalg.cholesky(a11, symmetrize_input=False)
    i11 = lax.linalg.triangular_solve(l11, eye, left_side=True, lower=True)
    l21 = jnp.dot(a21, i11.T, precision=HIGHEST)
    s = a22 - jnp.dot(l21, l21.T, precision=HIGHEST)
    l22 = lax.linalg.cholesky(s, symmetrize_input=False)
    i22 = lax.linalg.triangular_solve(l22, eye, left_side=True, lower=True)
    i21 = -jnp.dot(i22, jnp.dot(l21, i11, precision=HIGHEST), precision=HIGHEST)
    z = jnp.zeros((h, h), jnp.float32)
    lower = jnp.block([[l11, z], [l21, l22]])
    inverse = jnp.block([[i11, z], [i21, i22]])
    return lower, inverse


def per_device(stationary, rotor_rows, owners, counts, omega):
    n_rows = lax.axis_size("rows")
    n_grp = lax.axis_size("grp")
    rot_dev = rotor_rows.shape[0]
    stat_dev = stationary.shape[0]
    total = n_grp * n_rows * (stat_dev + rot_dev)
    targets = owners[:, 0]
    live = lax.iota(jnp.int32, rot_dev) < counts[0]
    onehot = ((targets[:, None] == lax.iota(jnp.int32, n_rows)[None, :]) & live[:, None]).astype(
        jnp.int32
    )
    rank = jnp.sum((jnp.cumsum(onehot, axis=0) - onehot) * onehot, axis=1)
    slot = jnp.where(live, targets * CAP + rank, -1)
    select = (lax.iota(jnp.int32, n_rows * CAP)[:, None] == slot[None, :]).astype(jnp.bfloat16)

    sketch_stat = sketch_block(stationary, omega)
    sketch_rot = sketch_block(rotor_rows, omega)
    rot_live = jnp.where(live[:, None], sketch_rot, jnp.zeros_like(sketch_rot))

    dims = (((0,), (0,)), ((), ()))
    gram = lax.dot_general(sketch_stat, sketch_stat, dims, preferred_element_type=jnp.float32)
    gram = gram + lax.dot_general(rot_live, rot_live, dims, preferred_element_type=jnp.float32)
    gram = gram / total

    outgoing = jnp.dot(select, sketch_rot, preferred_element_type=jnp.float32).astype(jnp.bfloat16)
    outgoing = outgoing.reshape(n_rows, CAP, -1)
    arrived = lax.all_to_all(outgoing, "rows", split_axis=0, concat_axis=0, tiled=True)
    arrived = arrived.reshape(n_rows * CAP, -1)

    gram = unpack_sym(all_sum(pack_sym(gram), n_grp * n_rows))
    lower, inverse = cholesky_and_inverse(gram)
    basis_stat = jnp.dot(
        sketch_stat.astype(jnp.float32), inverse.T, precision=HIGHEST
    ).astype(jnp.bfloat16)
    basis_rot = jnp.dot(arrived.astype(jnp.float32), inverse.T, precision=HIGHEST).astype(
        jnp.bfloat16
    )
    return (basis_stat, basis_rot, lower.T)


def solution(mesh):
    return jax.shard_map(
        per_device,
        mesh=mesh,
        in_specs=(
            P(("grp", "rows"), None),
            P(("grp", "rows"), None),
            P(("grp", "rows"), None),
            P(("grp", "rows")),
            P(),
        ),
        out_specs=(P(("grp", "rows"), None), P(("grp", "rows"), None), P()),
        check_vma=False,
    )
```

```python
import jax
import jax.numpy as jnp
from jax import lax
from jax.sharding import PartitionSpec as P

CAP = 6
AXES = ("grp", "rows")
HIGHEST = lax.Precision.HIGHEST


def sketch_block(block, omega):
    return jnp.dot(block, omega, preferred_element_type=jnp.float32).astype(jnp.bfloat16)


def pack_sym(g):
    h = g.shape[0] // 2
    i = lax.broadcasted_iota(jnp.int32, (h, h), 0)
    j = lax.broadcasted_iota(jnp.int32, (h, h), 1)
    a, b, c = g[:h, :h], g[h:, :h], g[h:, h:]
    m = jnp.where(i >= j, a, c)
    diag_c = jnp.sum(jnp.where(i == j, c, 0.0), axis=0, keepdims=True)
    return jnp.concatenate([b, m, diag_c], axis=0)


def unpack_sym(p):
    h = p.shape[1]
    b, m, diag_c = p[:h], p[h : 2 * h], p[2 * h :]
    i = lax.broadcasted_iota(jnp.int32, (h, h), 0)
    j = lax.broadcasted_iota(jnp.int32, (h, h), 1)
    mt = m.T
    a = jnp.where(i >= j, m, mt)
    c = jnp.where(i < j, m, jnp.where(i > j, mt, diag_c))
    return jnp.concatenate(
        [jnp.concatenate([a, b.T], axis=1), jnp.concatenate([b, c], axis=1)], axis=0
    )


def all_sum_and_route(x, held, n, n_rows):
    bits = n.bit_length() - 1
    row_bits = n_rows.bit_length() - 1
    me = lax.axis_index(AXES)
    width = x.shape[1]
    for b in reversed(range(bits)):
        perm = [(i, i ^ (1 << b)) for i in range(n)]
        if b >= row_bits:
            x = x + lax.ppermute(x, AXES, perm)
            continue
        parts = held.reshape((n_rows >> (b + 1), 2, 1 << b) + held.shape[1:])
        mine = (me >> b) & 1
        keep = jnp.where(mine == 0, parts[:, 0], parts[:, 1])
        away = jnp.where(mine == 0, parts[:, 1], parts[:, 0])
        packet = jnp.concatenate([x, away.astype(jnp.float32).reshape(-1, width)], axis=0)
        got = lax.ppermute(packet, AXES, perm)
        x = x + got[: x.shape[0]]
        came = got[x.shape[0] :].reshape(away.shape).astype(held.dtype)
        lo = jnp.where(mine == 0, keep, came)
        hi = jnp.where(mine == 0, came, keep)
        held = jnp.stack([lo, hi], axis=1).reshape(held.shape)
    return x, held


def cholesky_and_inverse(g):
    k = g.shape[0]
    h = k // 2
    a11, a21, a22 = g[:h, :h], g[h:, :h], g[h:, h:]
    eye = jnp.eye(h, dtype=jnp.float32)
    l11 = lax.linalg.cholesky(a11, symmetrize_input=False)
    i11 = lax.linalg.triangular_solve(l11, eye, left_side=True, lower=True)
    l21 = jnp.dot(a21, i11.T, precision=HIGHEST)
    s = a22 - jnp.dot(l21, l21.T, precision=HIGHEST)
    l22 = lax.linalg.cholesky(s, symmetrize_input=False)
    i22 = lax.linalg.triangular_solve(l22, eye, left_side=True, lower=True)
    i21 = -jnp.dot(i22, jnp.dot(l21, i11, precision=HIGHEST), precision=HIGHEST)
    z = jnp.zeros((h, h), jnp.float32)
    lower = jnp.block([[l11, z], [l21, l22]])
    inverse = jnp.block([[i11, z], [i21, i22]])
    return lower, inverse


def per_device(stationary, rotor_rows, owners, counts, omega):
    n_rows = lax.axis_size("rows")
    n_grp = lax.axis_size("grp")
    rot_dev = rotor_rows.shape[0]
    stat_dev = stationary.shape[0]
    total = n_grp * n_rows * (stat_dev + rot_dev)
    k = omega.shape[1]
    targets = owners[:, 0]
    live = lax.iota(jnp.int32, rot_dev) < counts[0]
    onehot = ((targets[:, None] == lax.iota(jnp.int32, n_rows)[None, :]) & live[:, None]).astype(
        jnp.int32
    )
    rank = jnp.sum((jnp.cumsum(onehot, axis=0) - onehot) * onehot, axis=1)
    slot = jnp.where(live, targets * CAP + rank, -1)
    select = (lax.iota(jnp.int32, n_rows * CAP)[:, None] == slot[None, :]).astype(jnp.bfloat16)

    sketch_stat = sketch_block(stationary, omega)
    sketch_rot = sketch_block(rotor_rows, omega)
    rot_live = jnp.where(live[:, None], sketch_rot, jnp.zeros_like(sketch_rot))

    dims = (((0,), (0,)), ((), ()))
    gram = lax.dot_general(sketch_stat, sketch_stat, dims, preferred_element_type=jnp.float32)
    gram = gram + lax.dot_general(rot_live, rot_live, dims, preferred_element_type=jnp.float32)
    gram = gram / total

    outgoing = jnp.dot(select, sketch_rot, preferred_element_type=jnp.float32).astype(jnp.bfloat16)
    outgoing = outgoing.reshape(n_rows, CAP, -1)
    packed = pack_sym(gram)
    n = n_grp * n_rows
    if n & (n - 1) or n_rows & (n_rows - 1) or (CAP * k) % packed.shape[1]:
        arrived = lax.all_to_all(outgoing, "rows", split_axis=0, concat_axis=0, tiled=True)
        packed = lax.psum(packed, AXES)
    else:
        packed, arrived = all_sum_and_route(packed, outgoing, n, n_rows)
    arrived = arrived.reshape(n_rows * CAP, -1)
    gram = unpack_sym(packed)
    lower, inverse = cholesky_and_inverse(gram)
    basis_stat = jnp.dot(
        sketch_stat.astype(jnp.float32), inverse.T, precision=HIGHEST
    ).astype(jnp.bfloat16)
    basis_rot = jnp.dot(arrived.astype(jnp.float32), inverse.T, precision=HIGHEST).astype(
        jnp.bfloat16
    )
    return (basis_stat, basis_rot, lower.T)


def solution(mesh):
    return jax.shard_map(
        per_device,
        mesh=mesh,
        in_specs=(
            P(("grp", "rows"), None),
            P(("grp", "rows"), None),
            P(("grp", "rows"), None),
            P(("grp", "rows")),
            P(),
        ),
        out_specs=(P(("grp", "rows"), None), P(("grp", "rows"), None), P()),
        check_vma=False,
    )
```

```python
import functools

import jax
import jax.numpy as jnp
from jax import lax
from jax.experimental import pallas as pl
from jax.experimental.pallas import tpu as pltpu
from jax.sharding import PartitionSpec as P

CAP = 6
AXES = ("grp", "rows")
HIGHEST = lax.Precision.HIGHEST


def sketch_block(block, omega):
    return jnp.dot(block, omega, preferred_element_type=jnp.float32).astype(jnp.bfloat16)


def pack_sym(g):
    h = g.shape[0] // 2
    i = lax.broadcasted_iota(jnp.int32, (h, h), 0)
    j = lax.broadcasted_iota(jnp.int32, (h, h), 1)
    a, b, c = g[:h, :h], g[h:, :h], g[h:, h:]
    m = jnp.where(i >= j, a, c)
    diag_c = jnp.sum(jnp.where(i == j, c, 0.0), axis=0, keepdims=True)
    return jnp.concatenate([b, m, diag_c], axis=0)


def unpack_sym(p):
    h = p.shape[1]
    b, m, diag_c = p[:h], p[h : 2 * h], p[2 * h :]
    i = lax.broadcasted_iota(jnp.int32, (h, h), 0)
    j = lax.broadcasted_iota(jnp.int32, (h, h), 1)
    mt = m.T
    a = jnp.where(i >= j, m, mt)
    c = jnp.where(i < j, m, jnp.where(i > j, mt, diag_c))
    return jnp.concatenate(
        [jnp.concatenate([a, b.T], axis=1), jnp.concatenate([b, c], axis=1)], axis=0
    )


def all_sum_and_route(x, held, n, n_rows):
    bits = n.bit_length() - 1
    row_bits = n_rows.bit_length() - 1
    me = lax.axis_index(AXES)
    width = x.shape[1]
    for b in reversed(range(bits)):
        perm = [(i, i ^ (1 << b)) for i in range(n)]
        if b >= row_bits:
            x = x + lax.ppermute(x, AXES, perm)
            continue
        parts = held.reshape((n_rows >> (b + 1), 2, 1 << b) + held.shape[1:])
        mine = (me >> b) & 1
        keep = jnp.where(mine == 0, parts[:, 0], parts[:, 1])
        away = jnp.where(mine == 0, parts[:, 1], parts[:, 0])
        packet = jnp.concatenate([x, away.astype(jnp.float32).reshape(-1, width)], axis=0)
        got = lax.ppermute(packet, AXES, perm)
        x = x + got[: x.shape[0]]
        came = got[x.shape[0] :].reshape(away.shape).astype(held.dtype)
        lo = jnp.where(mine == 0, keep, came)
        hi = jnp.where(mine == 0, came, keep)
        held = jnp.stack([lo, hi], axis=1).reshape(held.shape)
    return x, held


def _chol_kernel(g_ref, u_ref, r_ref, b_ref, *, panel):
    k = g_ref.shape[0]
    w = 2 * k
    kp = ((k + 127) // 128) * 128
    rows = lax.broadcasted_iota(jnp.int32, (k, k), 0)
    cols = lax.broadcasted_iota(jnp.int32, (k, k), 1)
    b_ref[:, :k] = g_ref[...]
    b_ref[:, k:] = jnp.where(rows == cols, 1.0, 0.0).astype(jnp.float32)
    sub = lax.broadcasted_iota(jnp.int32, (panel, w), 0)
    lane = lax.broadcasted_iota(jnp.int32, (panel, w), 1)

    def step(p, carry):
        base = pl.multiple_of(p * panel, 8)
        pan = b_ref[pl.ds(base, panel), :]
        for r in range(panel):
            row = pan[r : r + 1, :]
            col = jnp.sum(jnp.where(lane == base + r, pan, 0.0), axis=1, keepdims=True)
            s = lax.rsqrt(col[r : r + 1, :])
            v = row * s
            pan = jnp.where(sub == r, v, jnp.where(sub > r, pan - (col * s) * v, pan))
        pan = jnp.where((lane < k) & (lane < base + sub), 0.0, pan)
        b_ref[pl.ds(base, panel), :] = pan
        part = jnp.where((lane >= base + panel) & (lane < k), pan, 0.0)[:, :kp]
        upd = lax.dot_general(
            part, pan, (((0,), (0,)), ((), ())), precision=HIGHEST, preferred_element_type=jnp.float32
        )
        b_ref[...] = b_ref[...] - upd[:k]
        return carry

    lax.fori_loop(0, k // panel, step, 0)
    u_ref[...] = b_ref[:, :k]
    r_ref[...] = b_ref[:, k:]


def cholesky_and_inverse(g):
    k = g.shape[0]
    panel = next((p for p in (96, 64, 48, 32, 16, 8) if k % p == 0), None)
    if panel is None:
        lower = jnp.linalg.cholesky(g)
        eye = jnp.eye(k, dtype=jnp.float32)
        return lower.T, lax.linalg.triangular_solve(lower, eye, left_side=True, lower=True)
    vmem = pl.BlockSpec(memory_space=pltpu.VMEM)
    out = jax.ShapeDtypeStruct((k, k), jnp.float32)
    return pl.pallas_call(
        functools.partial(_chol_kernel, panel=panel),
        out_shape=(out, out),
        in_specs=[vmem],
        out_specs=(vmem, vmem),
        scratch_shapes=[pltpu.VMEM((k, 2 * k), jnp.float32)],
    )(g)


def per_device(stationary, rotor_rows, owners, counts, omega):
    n_rows = lax.axis_size("rows")
    n_grp = lax.axis_size("grp")
    rot_dev = rotor_rows.shape[0]
    stat_dev = stationary.shape[0]
    total = n_grp * n_rows * (stat_dev + rot_dev)
    k = omega.shape[1]
    targets = owners[:, 0]
    live = lax.iota(jnp.int32, rot_dev) < counts[0]
    onehot = ((targets[:, None] == lax.iota(jnp.int32, n_rows)[None, :]) & live[:, None]).astype(
        jnp.int32
    )
    rank = jnp.sum((jnp.cumsum(onehot, axis=0) - onehot) * onehot, axis=1)
    slot = jnp.where(live, targets * CAP + rank, -1)
    select = (lax.iota(jnp.int32, n_rows * CAP)[:, None] == slot[None, :]).astype(jnp.bfloat16)

    sketch_stat = sketch_block(stationary, omega)
    sketch_rot = sketch_block(rotor_rows, omega)
    rot_live = jnp.where(live[:, None], sketch_rot, jnp.zeros_like(sketch_rot))

    dims = (((0,), (0,)), ((), ()))
    gram = lax.dot_general(sketch_stat, sketch_stat, dims, preferred_element_type=jnp.float32)
    gram = gram + lax.dot_general(rot_live, rot_live, dims, preferred_element_type=jnp.float32)
    gram = gram / total

    outgoing = jnp.dot(select, sketch_rot, preferred_element_type=jnp.float32).astype(jnp.bfloat16)
    outgoing = outgoing.reshape(n_rows, CAP, -1)
    packed = pack_sym(gram)
    n = n_grp * n_rows
    if n & (n - 1) or n_rows & (n_rows - 1) or (CAP * k) % packed.shape[1]:
        arrived = lax.all_to_all(outgoing, "rows", split_axis=0, concat_axis=0, tiled=True)
        packed = lax.psum(packed, AXES)
    else:
        packed, arrived = all_sum_and_route(packed, outgoing, n, n_rows)
    arrived = arrived.reshape(n_rows * CAP, -1)
    gram = unpack_sym(packed)
    upper, inverse = cholesky_and_inverse(gram)
    basis_stat = jnp.dot(
        sketch_stat.astype(jnp.float32), inverse.T, precision=HIGHEST
    ).astype(jnp.bfloat16)
    basis_rot = jnp.dot(arrived.astype(jnp.float32), inverse.T, precision=HIGHEST).astype(
        jnp.bfloat16
    )
    return (basis_stat, basis_rot, upper)


def solution(mesh):
    return jax.shard_map(
        per_device,
        mesh=mesh,
        in_specs=(
            P(("grp", "rows"), None),
            P(("grp", "rows"), None),
            P(("grp", "rows"), None),
            P(("grp", "rows")),
            P(),
        ),
        out_specs=(P(("grp", "rows"), None), P(("grp", "rows"), None), P()),
        check_vma=False,
    )
```

```python
import functools

import jax
import jax.numpy as jnp
from jax import lax
from jax.experimental import pallas as pl
from jax.experimental.pallas import tpu as pltpu
from jax.sharding import PartitionSpec as P

CAP = 6
AXES = ("grp", "rows")
HIGHEST = lax.Precision.HIGHEST


def sketch_block(block, omega):
    return jnp.dot(block, omega, preferred_element_type=jnp.float32).astype(jnp.bfloat16)


def pack_sym(g):
    h = g.shape[0] // 2
    i = lax.broadcasted_iota(jnp.int32, (h, h), 0)
    j = lax.broadcasted_iota(jnp.int32, (h, h), 1)
    a, b, c = g[:h, :h], g[h:, :h], g[h:, h:]
    m = jnp.where(i >= j, a, c)
    diag_c = jnp.sum(jnp.where(i == j, c, 0.0), axis=0, keepdims=True)
    return jnp.concatenate([b, m, diag_c], axis=0)


def unpack_sym(p):
    h = p.shape[1]
    b, m, diag_c = p[:h], p[h : 2 * h], p[2 * h :]
    i = lax.broadcasted_iota(jnp.int32, (h, h), 0)
    j = lax.broadcasted_iota(jnp.int32, (h, h), 1)
    mt = m.T
    a = jnp.where(i >= j, m, mt)
    c = jnp.where(i < j, m, jnp.where(i > j, mt, diag_c))
    return jnp.concatenate(
        [jnp.concatenate([a, b.T], axis=1), jnp.concatenate([b, c], axis=1)], axis=0
    )


def all_sum_and_route(x, held, n, n_rows):
    bits = n.bit_length() - 1
    row_bits = n_rows.bit_length() - 1
    me = lax.axis_index(AXES)
    width = x.shape[1]
    for b in reversed(range(bits)):
        perm = [(i, i ^ (1 << b)) for i in range(n)]
        if b >= row_bits:
            x = x + lax.ppermute(x, AXES, perm)
            continue
        parts = held.reshape((n_rows >> (b + 1), 2, 1 << b) + held.shape[1:])
        mine = (me >> b) & 1
        keep = jnp.where(mine == 0, parts[:, 0], parts[:, 1])
        away = jnp.where(mine == 0, parts[:, 1], parts[:, 0])
        packet = jnp.concatenate([x, away.astype(jnp.float32).reshape(-1, width)], axis=0)
        got = lax.ppermute(packet, AXES, perm)
        x = x + got[: x.shape[0]]
        came = got[x.shape[0] :].reshape(away.shape).astype(held.dtype)
        lo = jnp.where(mine == 0, keep, came)
        hi = jnp.where(mine == 0, came, keep)
        held = jnp.stack([lo, hi], axis=1).reshape(held.shape)
    return x, held


def _chol_kernel(g_ref, u_ref, r_ref, b_ref, *, panel):
    k = g_ref.shape[0]
    w = 2 * k
    kp = ((k + 127) // 128) * 128
    rows = lax.broadcasted_iota(jnp.int32, (k, k), 0)
    cols = lax.broadcasted_iota(jnp.int32, (k, k), 1)
    b_ref[:, :k] = g_ref[...]
    b_ref[:, k:] = jnp.where(rows == cols, 1.0, 0.0).astype(jnp.float32)
    for p in range(k // panel):
        base = p * panel
        end = base + panel
        pan = b_ref[base:end, :]
        for r in range(0, panel, 2):
            piv = base + r
            t0 = (piv // 128) * 128
            s0 = (r // 8) * 8
            top, low = pan[:s0], pan[s0:]
            m = panel - s0
            i0, i1 = r - s0, r + 1 - s0
            row0, row1 = low[i0 : i0 + 1], low[i1 : i1 + 1]
            lane = lax.broadcasted_iota(jnp.int32, (m, 128), 1) + t0
            blk = low[:, t0 : t0 + 128]
            c0 = jnp.sum(jnp.where(lane == piv, blk, 0.0), axis=1, keepdims=True)
            c1 = jnp.sum(jnp.where(lane == piv + 1, blk, 0.0), axis=1, keepdims=True)
            s1 = lax.rsqrt(c0[i0 : i0 + 1])
            v1 = row0 * s1
            coef1 = c0 * s1
            l = coef1[i1 : i1 + 1]
            c1p = c1 - coef1 * l
            s2 = lax.rsqrt(c1p[i1 : i1 + 1])
            v2 = (row1 - l * v1) * s2
            coef2 = c1p * s2
            sub = lax.broadcasted_iota(jnp.int32, (m, w), 0) + s0
            low = jnp.where(
                sub > r + 1,
                low - coef1 * v1 - coef2 * v2,
                jnp.where(sub == r, v1, jnp.where(sub == r + 1, v2, low)),
            )
            pan = jnp.concatenate([top, low], axis=0) if s0 else low
        sub = lax.broadcasted_iota(jnp.int32, pan.shape, 0) + base
        lane = lax.broadcasted_iota(jnp.int32, pan.shape, 1)
        pan = jnp.where((lane < k) & (lane < sub), 0.0, pan)
        b_ref[base:end, :] = pan
        if end < k:
            part = jnp.where((lane >= end) & (lane < k), pan, 0.0)[:, :kp]
            upd = lax.dot_general(
                part, pan, (((0,), (0,)), ((), ())), precision=HIGHEST,
                preferred_element_type=jnp.float32,
            )
            b_ref[end:, :] = b_ref[end:, :] - upd[end:k]
    u_ref[...] = b_ref[:, :k]
    r_ref[...] = b_ref[:, k:]


def cholesky_and_inverse(g):
    k = g.shape[0]
    panel = next((p for p in (96, 64, 48, 32, 16, 8) if k % p == 0), None)
    if panel is None:
        lower = jnp.linalg.cholesky(g)
        eye = jnp.eye(k, dtype=jnp.float32)
        return lower.T, lax.linalg.triangular_solve(lower, eye, left_side=True, lower=True)
    vmem = pl.BlockSpec(memory_space=pltpu.VMEM)
    out = jax.ShapeDtypeStruct((k, k), jnp.float32)
    return pl.pallas_call(
        functools.partial(_chol_kernel, panel=panel),
        out_shape=(out, out),
        in_specs=[vmem],
        out_specs=(vmem, vmem),
        scratch_shapes=[pltpu.VMEM((k, 2 * k), jnp.float32)],
    )(g)


def per_device(stationary, rotor_rows, owners, counts, omega):
    n_rows = lax.axis_size("rows")
    n_grp = lax.axis_size("grp")
    rot_dev = rotor_rows.shape[0]
    stat_dev = stationary.shape[0]
    total = n_grp * n_rows * (stat_dev + rot_dev)
    k = omega.shape[1]
    targets = owners[:, 0]
    live = lax.iota(jnp.int32, rot_dev) < counts[0]
    onehot = ((targets[:, None] == lax.iota(jnp.int32, n_rows)[None, :]) & live[:, None]).astype(
        jnp.int32
    )
    rank = jnp.sum((jnp.cumsum(onehot, axis=0) - onehot) * onehot, axis=1)
    slot = jnp.where(live, targets * CAP + rank, -1)
    select = (lax.iota(jnp.int32, n_rows * CAP)[:, None] == slot[None, :]).astype(jnp.bfloat16)

    sketch_stat = sketch_block(stationary, omega)
    sketch_rot = sketch_block(rotor_rows, omega)
    rot_live = jnp.where(live[:, None], sketch_rot, jnp.zeros_like(sketch_rot))

    dims = (((0,), (0,)), ((), ()))
    gram = lax.dot_general(sketch_stat, sketch_stat, dims, preferred_element_type=jnp.float32)
    gram = gram + lax.dot_general(rot_live, rot_live, dims, preferred_element_type=jnp.float32)
    gram = gram / total

    outgoing = jnp.dot(select, sketch_rot, preferred_element_type=jnp.float32).astype(jnp.bfloat16)
    outgoing = outgoing.reshape(n_rows, CAP, -1)
    packed = pack_sym(gram)
    n = n_grp * n_rows
    if n & (n - 1) or n_rows & (n_rows - 1) or (CAP * k) % packed.shape[1]:
        arrived = lax.all_to_all(outgoing, "rows", split_axis=0, concat_axis=0, tiled=True)
        packed = lax.psum(packed, AXES)
    else:
        packed, arrived = all_sum_and_route(packed, outgoing, n, n_rows)
    arrived = arrived.reshape(n_rows * CAP, -1)
    gram = unpack_sym(packed)
    upper, inverse = cholesky_and_inverse(gram)
    basis_stat = jnp.dot(
        sketch_stat.astype(jnp.float32), inverse.T, precision=HIGHEST
    ).astype(jnp.bfloat16)
    basis_rot = jnp.dot(arrived.astype(jnp.float32), inverse.T, precision=HIGHEST).astype(
        jnp.bfloat16
    )
    return (basis_stat, basis_rot, upper)


def solution(mesh):
    return jax.shard_map(
        per_device,
        mesh=mesh,
        in_specs=(
            P(("grp", "rows"), None),
            P(("grp", "rows"), None),
            P(("grp", "rows"), None),
            P(("grp", "rows")),
            P(),
        ),
        out_specs=(P(("grp", "rows"), None), P(("grp", "rows"), None), P()),
        check_vma=False,
    )
```

```python
import functools

import jax
import jax.numpy as jnp
from jax import lax
from jax.experimental import pallas as pl
from jax.experimental.pallas import tpu as pltpu
from jax.sharding import PartitionSpec as P

CAP = 6
AXES = ("grp", "rows")
HIGHEST = lax.Precision.HIGHEST
GROUP = 8


def sketch_block(block, omega):
    return jnp.dot(block, omega, preferred_element_type=jnp.float32).astype(jnp.bfloat16)


def pack_sym(g):
    h = g.shape[0] // 2
    i = lax.broadcasted_iota(jnp.int32, (h, h), 0)
    j = lax.broadcasted_iota(jnp.int32, (h, h), 1)
    a, b, c = g[:h, :h], g[h:, :h], g[h:, h:]
    m = jnp.where(i >= j, a, c)
    diag_c = jnp.sum(jnp.where(i == j, c, 0.0), axis=0, keepdims=True)
    return jnp.concatenate([b, m, diag_c], axis=0)


def unpack_sym(p):
    h = p.shape[1]
    b, m, diag_c = p[:h], p[h : 2 * h], p[2 * h :]
    i = lax.broadcasted_iota(jnp.int32, (h, h), 0)
    j = lax.broadcasted_iota(jnp.int32, (h, h), 1)
    mt = m.T
    a = jnp.where(i >= j, m, mt)
    c = jnp.where(i < j, m, jnp.where(i > j, mt, diag_c))
    return jnp.concatenate(
        [jnp.concatenate([a, b.T], axis=1), jnp.concatenate([b, c], axis=1)], axis=0
    )


def all_sum_and_route(x, held, n, n_rows):
    bits = n.bit_length() - 1
    row_bits = n_rows.bit_length() - 1
    me = lax.axis_index(AXES)
    width = x.shape[1]
    for b in reversed(range(bits)):
        perm = [(i, i ^ (1 << b)) for i in range(n)]
        if b >= row_bits:
            x = x + lax.ppermute(x, AXES, perm)
            continue
        parts = held.reshape((n_rows >> (b + 1), 2, 1 << b) + held.shape[1:])
        mine = (me >> b) & 1
        keep = jnp.where(mine == 0, parts[:, 0], parts[:, 1])
        away = jnp.where(mine == 0, parts[:, 1], parts[:, 0])
        packet = jnp.concatenate([x, away.astype(jnp.float32).reshape(-1, width)], axis=0)
        got = lax.ppermute(packet, AXES, perm)
        x = x + got[: x.shape[0]]
        came = got[x.shape[0] :].reshape(away.shape).astype(held.dtype)
        lo = jnp.where(mine == 0, keep, came)
        hi = jnp.where(mine == 0, came, keep)
        held = jnp.stack([lo, hi], axis=1).reshape(held.shape)
    return x, held


def _chol_kernel(g_ref, u_ref, r_ref, b_ref, *, panel):
    k = g_ref.shape[0]
    w = 2 * k
    kp = ((k + 127) // 128) * 128
    rows = lax.broadcasted_iota(jnp.int32, (k, k), 0)
    cols = lax.broadcasted_iota(jnp.int32, (k, k), 1)
    b_ref[:, :k] = g_ref[...]
    b_ref[:, k:] = jnp.where(rows == cols, 1.0, 0.0).astype(jnp.float32)
    for p in range(k // panel):
        base = p * panel
        end = base + panel
        pan = b_ref[base:end, :]
        for r in range(0, panel, GROUP):
            piv = base + r
            t0 = (piv // 128) * 128
            top, low = pan[:r], pan[r:]
            m = panel - r
            lane = lax.broadcasted_iota(jnp.int32, (m, 128), 1) + t0
            blk = low[:, t0 : t0 + 128]
            cs = [
                jnp.sum(jnp.where(lane == piv + t, blk, 0.0), axis=1, keepdims=True)
                for t in range(GROUP)
            ]
            coefs, vs = [], []
            for t in range(GROUP):
                c, row = cs[t], low[t : t + 1]
                for u in range(t):
                    lu = coefs[u][t : t + 1]
                    c = c - coefs[u] * lu
                    row = row - lu * vs[u]
                s = lax.rsqrt(c[t : t + 1])
                vs.append(row * s)
                coefs.append(c * s)
            sub = lax.broadcasted_iota(jnp.int32, (m, w), 0)
            upd = low
            for t in range(GROUP):
                upd = upd - coefs[t] * vs[t]
            low = jnp.where(sub >= GROUP, upd, low)
            for t in range(GROUP):
                low = jnp.where(sub == t, vs[t], low)
            pan = jnp.concatenate([top, low], axis=0) if r else low
        sub = lax.broadcasted_iota(jnp.int32, pan.shape, 0) + base
        lane = lax.broadcasted_iota(jnp.int32, pan.shape, 1)
        pan = jnp.where((lane < k) & (lane < sub), 0.0, pan)
        b_ref[base:end, :] = pan
        if end < k:
            part = jnp.where((lane >= end) & (lane < k), pan, 0.0)[:, :kp]
            upd = lax.dot_general(
                part, pan, (((0,), (0,)), ((), ())), precision=HIGHEST,
                preferred_element_type=jnp.float32,
            )
            b_ref[end:, :] = b_ref[end:, :] - upd[end:k]
    u_ref[...] = b_ref[:, :k]
    r_ref[...] = b_ref[:, k:]


def cholesky_and_inverse(g):
    k = g.shape[0]
    panel = next((p for p in (96, 64, 48, 32, 16, 8) if k % p == 0), None)
    if panel is None:
        lower = jnp.linalg.cholesky(g)
        eye = jnp.eye(k, dtype=jnp.float32)
        return lower.T, lax.linalg.triangular_solve(lower, eye, left_side=True, lower=True)
    vmem = pl.BlockSpec(memory_space=pltpu.VMEM)
    out = jax.ShapeDtypeStruct((k, k), jnp.float32)
    return pl.pallas_call(
        functools.partial(_chol_kernel, panel=panel),
        out_shape=(out, out),
        in_specs=[vmem],
        out_specs=(vmem, vmem),
        scratch_shapes=[pltpu.VMEM((k, 2 * k), jnp.float32)],
    )(g)


def per_device(stationary, rotor_rows, owners, counts, omega):
    n_rows = lax.axis_size("rows")
    n_grp = lax.axis_size("grp")
    rot_dev = rotor_rows.shape[0]
    stat_dev = stationary.shape[0]
    total = n_grp * n_rows * (stat_dev + rot_dev)
    k = omega.shape[1]
    targets = owners[:, 0]
    live = lax.iota(jnp.int32, rot_dev) < counts[0]
    onehot = ((targets[:, None] == lax.iota(jnp.int32, n_rows)[None, :]) & live[:, None]).astype(
        jnp.int32
    )
    rank = jnp.sum((jnp.cumsum(onehot, axis=0) - onehot) * onehot, axis=1)
    slot = jnp.where(live, targets * CAP + rank, -1)
    select = (lax.iota(jnp.int32, n_rows * CAP)[:, None] == slot[None, :]).astype(jnp.bfloat16)

    sketch_stat = sketch_block(stationary, omega)
    sketch_rot = sketch_block(rotor_rows, omega)
    rot_live = jnp.where(live[:, None], sketch_rot, jnp.zeros_like(sketch_rot))

    dims = (((0,), (0,)), ((), ()))
    gram = lax.dot_general(sketch_stat, sketch_stat, dims, preferred_element_type=jnp.float32)
    gram = gram + lax.dot_general(rot_live, rot_live, dims, preferred_element_type=jnp.float32)
    gram = gram / total

    outgoing = jnp.dot(select, sketch_rot, preferred_element_type=jnp.float32).astype(jnp.bfloat16)
    outgoing = outgoing.reshape(n_rows, CAP, -1)
    packed = pack_sym(gram)
    n = n_grp * n_rows
    if n & (n - 1) or n_rows & (n_rows - 1) or (CAP * k) % packed.shape[1]:
        arrived = lax.all_to_all(outgoing, "rows", split_axis=0, concat_axis=0, tiled=True)
        packed = lax.psum(packed, AXES)
    else:
        packed, arrived = all_sum_and_route(packed, outgoing, n, n_rows)
    arrived = arrived.reshape(n_rows * CAP, -1)
    gram = unpack_sym(packed)
    upper, inverse = cholesky_and_inverse(gram)
    basis_stat = jnp.dot(
        sketch_stat.astype(jnp.float32), inverse.T, precision=HIGHEST
    ).astype(jnp.bfloat16)
    basis_rot = jnp.dot(arrived.astype(jnp.float32), inverse.T, precision=HIGHEST).astype(
        jnp.bfloat16
    )
    return (basis_stat, basis_rot, upper)


def solution(mesh):
    return jax.shard_map(
        per_device,
        mesh=mesh,
        in_specs=(
            P(("grp", "rows"), None),
            P(("grp", "rows"), None),
            P(("grp", "rows"), None),
            P(("grp", "rows")),
            P(),
        ),
        out_specs=(P(("grp", "rows"), None), P(("grp", "rows"), None), P()),
        check_vma=False,
    )
```

```python
import functools

import jax
import jax.numpy as jnp
from jax import lax
from jax.experimental import pallas as pl
from jax.experimental.pallas import tpu as pltpu
from jax.sharding import PartitionSpec as P

CAP = 6
AXES = ("grp", "rows")
HIGHEST = lax.Precision.HIGHEST
GROUP = 8


def sketch_block(block, omega):
    return jnp.dot(block, omega, preferred_element_type=jnp.float32).astype(jnp.bfloat16)


def pack_sym(g):
    h = g.shape[0] // 2
    i = lax.broadcasted_iota(jnp.int32, (h, h), 0)
    j = lax.broadcasted_iota(jnp.int32, (h, h), 1)
    a, b, c = g[:h, :h], g[h:, :h], g[h:, h:]
    m = jnp.where(i >= j, a, c)
    diag_c = jnp.sum(jnp.where(i == j, c, 0.0), axis=0, keepdims=True)
    return jnp.concatenate([b, m, diag_c], axis=0)


def unpack_sym(p):
    h = p.shape[1]
    b, m, diag_c = p[:h], p[h : 2 * h], p[2 * h :]
    i = lax.broadcasted_iota(jnp.int32, (h, h), 0)
    j = lax.broadcasted_iota(jnp.int32, (h, h), 1)
    mt = m.T
    a = jnp.where(i >= j, m, mt)
    c = jnp.where(i < j, m, jnp.where(i > j, mt, diag_c))
    return jnp.concatenate(
        [jnp.concatenate([a, b.T], axis=1), jnp.concatenate([b, c], axis=1)], axis=0
    )


def all_sum_and_route(x, held, n, n_rows):
    bits = n.bit_length() - 1
    row_bits = n_rows.bit_length() - 1
    me = lax.axis_index(AXES)
    width = x.shape[1]
    for b in reversed(range(bits)):
        perm = [(i, i ^ (1 << b)) for i in range(n)]
        if b >= row_bits:
            x = x + lax.ppermute(x, AXES, perm)
            continue
        parts = held.reshape((n_rows >> (b + 1), 2, 1 << b) + held.shape[1:])
        mine = (me >> b) & 1
        keep = jnp.where(mine == 0, parts[:, 0], parts[:, 1])
        away = jnp.where(mine == 0, parts[:, 1], parts[:, 0])
        packet = jnp.concatenate([x, away.astype(jnp.float32).reshape(-1, width)], axis=0)
        got = lax.ppermute(packet, AXES, perm)
        x = x + got[: x.shape[0]]
        came = got[x.shape[0] :].reshape(away.shape).astype(held.dtype)
        lo = jnp.where(mine == 0, keep, came)
        hi = jnp.where(mine == 0, came, keep)
        held = jnp.stack([lo, hi], axis=1).reshape(held.shape)
    return x, held


def _chol_kernel(g_ref, u_ref, hi_ref, mid_ref, lo_ref, b_ref, *, panel):
    k = g_ref.shape[0]
    w = 2 * k
    kp = ((k + 127) // 128) * 128
    rows = lax.broadcasted_iota(jnp.int32, (k, k), 0)
    cols = lax.broadcasted_iota(jnp.int32, (k, k), 1)
    b_ref[:, :k] = g_ref[...]
    b_ref[:, k:] = jnp.where(rows == cols, 1.0, 0.0).astype(jnp.float32)
    for p in range(k // panel):
        base = p * panel
        end = base + panel
        pan = b_ref[base:end, :]
        for r in range(0, panel, GROUP):
            piv = base + r
            t0 = (piv // 128) * 128
            top, low = pan[:r], pan[r:]
            m = panel - r
            lane = lax.broadcasted_iota(jnp.int32, (m, 128), 1) + t0
            blk = low[:, t0 : t0 + 128]
            cs = [
                jnp.sum(jnp.where(lane == piv + t, blk, 0.0), axis=1, keepdims=True)
                for t in range(GROUP)
            ]
            coefs, vs = [], []
            for t in range(GROUP):
                c, row = cs[t], low[t : t + 1]
                for u in range(t):
                    lu = coefs[u][t : t + 1]
                    c = c - coefs[u] * lu
                    row = row - lu * vs[u]
                s = lax.rsqrt(c[t : t + 1])
                vs.append(row * s)
                coefs.append(c * s)
            sub = lax.broadcasted_iota(jnp.int32, (m, w), 0)
            upd = low
            for t in range(GROUP):
                upd = upd - coefs[t] * vs[t]
            low = jnp.where(sub >= GROUP, upd, low)
            for t in range(GROUP):
                low = jnp.where(sub == t, vs[t], low)
            pan = jnp.concatenate([top, low], axis=0) if r else low
        sub = lax.broadcasted_iota(jnp.int32, pan.shape, 0) + base
        lane = lax.broadcasted_iota(jnp.int32, pan.shape, 1)
        pan = jnp.where((lane < k) & (lane < sub), 0.0, pan)
        b_ref[base:end, :] = pan
        if end < k:
            part = jnp.where((lane >= end) & (lane < k), pan, 0.0)[:, :kp]
            upd = lax.dot_general(
                part, pan, (((0,), (0,)), ((), ())), precision=HIGHEST,
                preferred_element_type=jnp.float32,
            )
            b_ref[end:, :] = b_ref[end:, :] - upd[end:k]
    u_ref[...] = b_ref[:, :k]
    rest = b_ref[:, k:]
    for part in (hi_ref, mid_ref, lo_ref):
        term = rest.astype(jnp.bfloat16)
        part[...] = term
        rest = rest - term.astype(jnp.float32)


def cholesky_and_inverse(g):
    k = g.shape[0]
    panel = next((p for p in (96, 64, 48, 32, 16, 8) if k % p == 0), None)
    if panel is None:
        lower = jnp.linalg.cholesky(g)
        eye = jnp.eye(k, dtype=jnp.float32)
        inverse = lax.linalg.triangular_solve(lower, eye, left_side=True, lower=True)
        return lower.T, (inverse,)
    vmem = pl.BlockSpec(memory_space=pltpu.VMEM)
    half = jax.ShapeDtypeStruct((k, k), jnp.bfloat16)
    upper, *parts = pl.pallas_call(
        functools.partial(_chol_kernel, panel=panel),
        out_shape=(jax.ShapeDtypeStruct((k, k), jnp.float32), half, half, half),
        in_specs=[vmem],
        out_specs=(vmem, vmem, vmem, vmem),
        scratch_shapes=[pltpu.VMEM((k, 2 * k), jnp.float32)],
    )(g)
    return upper, tuple(parts)


def apply_inverse(y, parts):
    dims = (((1,), (1,)), ((), ()))
    out = None
    for part in parts:
        if part.dtype == jnp.float32:
            term = jnp.dot(y.astype(jnp.float32), part.T, precision=HIGHEST)
        else:
            term = lax.dot_general(y, part, dims, preferred_element_type=jnp.float32)
        out = term if out is None else out + term
    return out.astype(jnp.bfloat16)


def per_device(stationary, rotor_rows, owners, counts, omega):
    n_rows = lax.axis_size("rows")
    n_grp = lax.axis_size("grp")
    rot_dev = rotor_rows.shape[0]
    stat_dev = stationary.shape[0]
    total = n_grp * n_rows * (stat_dev + rot_dev)
    k = omega.shape[1]
    targets = owners[:, 0]
    live = lax.iota(jnp.int32, rot_dev) < counts[0]
    onehot = ((targets[:, None] == lax.iota(jnp.int32, n_rows)[None, :]) & live[:, None]).astype(
        jnp.int32
    )
    rank = jnp.sum((jnp.cumsum(onehot, axis=0) - onehot) * onehot, axis=1)
    slot = jnp.where(live, targets * CAP + rank, -1)
    select = (lax.iota(jnp.int32, n_rows * CAP)[:, None] == slot[None, :]).astype(jnp.bfloat16)

    sketch_stat = sketch_block(stationary, omega)
    sketch_rot = sketch_block(rotor_rows, omega)
    rot_live = jnp.where(live[:, None], sketch_rot, jnp.zeros_like(sketch_rot))

    dims = (((0,), (0,)), ((), ()))
    gram = lax.dot_general(sketch_stat, sketch_stat, dims, preferred_element_type=jnp.float32)
    gram = gram + lax.dot_general(rot_live, rot_live, dims, preferred_element_type=jnp.float32)
    gram = gram / total

    outgoing = jnp.dot(select, sketch_rot, preferred_element_type=jnp.float32).astype(jnp.bfloat16)
    outgoing = outgoing.reshape(n_rows, CAP, -1)
    packed = pack_sym(gram)
    n = n_grp * n_rows
    if n & (n - 1) or n_rows & (n_rows - 1) or (CAP * k) % packed.shape[1]:
        arrived = lax.all_to_all(outgoing, "rows", split_axis=0, concat_axis=0, tiled=True)
        packed = lax.psum(packed, AXES)
    else:
        packed, arrived = all_sum_and_route(packed, outgoing, n, n_rows)
    arrived = arrived.reshape(n_rows * CAP, -1)
    gram = unpack_sym(packed)
    upper, parts = cholesky_and_inverse(gram)
    basis_stat = apply_inverse(sketch_stat, parts)
    basis_rot = apply_inverse(arrived, parts)
    return (basis_stat, basis_rot, upper)


def solution(mesh):
    return jax.shard_map(
        per_device,
        mesh=mesh,
        in_specs=(
            P(("grp", "rows"), None),
            P(("grp", "rows"), None),
            P(("grp", "rows"), None),
            P(("grp", "rows")),
            P(),
        ),
        out_specs=(P(("grp", "rows"), None), P(("grp", "rows"), None), P()),
        check_vma=False,
    )
```

```python
import functools

import jax
import jax.numpy as jnp
from jax import lax
from jax.experimental import pallas as pl
from jax.experimental.pallas import tpu as pltpu
from jax.sharding import PartitionSpec as P

CAP = 6
AXES = ("grp", "rows")
HIGHEST = lax.Precision.HIGHEST
GROUP = 8


def sketch_block(block, omega):
    return jnp.dot(block, omega, preferred_element_type=jnp.float32).astype(jnp.bfloat16)


def pack_sym(g):
    h = g.shape[0] // 2
    i = lax.broadcasted_iota(jnp.int32, (h, h), 0)
    j = lax.broadcasted_iota(jnp.int32, (h, h), 1)
    a, b, c = g[:h, :h], g[h:, :h], g[h:, h:]
    m = jnp.where(i >= j, a, c)
    diag_c = jnp.sum(jnp.where(i == j, c, 0.0), axis=0, keepdims=True)
    return jnp.concatenate([b, m, diag_c], axis=0)


def unpack_sym(p):
    h = p.shape[1]
    b, m, diag_c = p[:h], p[h : 2 * h], p[2 * h :]
    i = lax.broadcasted_iota(jnp.int32, (h, h), 0)
    j = lax.broadcasted_iota(jnp.int32, (h, h), 1)
    mt = m.T
    a = jnp.where(i >= j, m, mt)
    c = jnp.where(i < j, m, jnp.where(i > j, mt, diag_c))
    return jnp.concatenate(
        [jnp.concatenate([a, b.T], axis=1), jnp.concatenate([b, c], axis=1)], axis=0
    )


def all_sum_and_route(x, held, n, n_rows):
    bits = n.bit_length() - 1
    row_bits = n_rows.bit_length() - 1
    me = lax.axis_index(AXES)
    width = x.shape[1]
    for b in reversed(range(bits)):
        perm = [(i, i ^ (1 << b)) for i in range(n)]
        if b >= row_bits:
            x = x + lax.ppermute(x, AXES, perm)
            continue
        parts = held.reshape((n_rows >> (b + 1), 2, 1 << b) + held.shape[1:])
        mine = (me >> b) & 1
        keep = jnp.where(mine == 0, parts[:, 0], parts[:, 1])
        away = jnp.where(mine == 0, parts[:, 1], parts[:, 0])
        packet = jnp.concatenate([x, away.astype(jnp.float32).reshape(-1, width)], axis=0)
        got = lax.ppermute(packet, AXES, perm)
        x = x + got[: x.shape[0]]
        came = got[x.shape[0] :].reshape(away.shape).astype(held.dtype)
        lo = jnp.where(mine == 0, keep, came)
        hi = jnp.where(mine == 0, came, keep)
        held = jnp.stack([lo, hi], axis=1).reshape(held.shape)
    return x, held


def _chol_kernel(g_ref, ys_ref, yr_ref, u_ref, bs_ref, br_ref, b_ref, *, panel):
    k = g_ref.shape[0]
    w = 2 * k
    kp = ((k + 127) // 128) * 128
    rows = lax.broadcasted_iota(jnp.int32, (k, k), 0)
    cols = lax.broadcasted_iota(jnp.int32, (k, k), 1)
    b_ref[:, :k] = g_ref[...]
    b_ref[:, k:] = jnp.where(rows == cols, 1.0, 0.0).astype(jnp.float32)
    for p in range(k // panel):
        base = p * panel
        end = base + panel
        pan = b_ref[base:end, :]
        for r in range(0, panel, GROUP):
            piv = base + r
            t0 = (piv // 128) * 128
            top, low = pan[:r], pan[r:]
            m = panel - r
            lane = lax.broadcasted_iota(jnp.int32, (m, 128), 1) + t0
            blk = low[:, t0 : t0 + 128]
            cs = [
                jnp.sum(jnp.where(lane == piv + t, blk, 0.0), axis=1, keepdims=True)
                for t in range(GROUP)
            ]
            coefs, vs = [], []
            for t in range(GROUP):
                c, row = cs[t], low[t : t + 1]
                for u in range(t):
                    lu = coefs[u][t : t + 1]
                    c = c - coefs[u] * lu
                    row = row - lu * vs[u]
                s = lax.rsqrt(c[t : t + 1])
                vs.append(row * s)
                coefs.append(c * s)
            sub = lax.broadcasted_iota(jnp.int32, (m, w), 0)
            upd = low
            for t in range(GROUP):
                upd = upd - coefs[t] * vs[t]
            low = jnp.where(sub >= GROUP, upd, low)
            for t in range(GROUP):
                low = jnp.where(sub == t, vs[t], low)
            pan = jnp.concatenate([top, low], axis=0) if r else low
        sub = lax.broadcasted_iota(jnp.int32, pan.shape, 0) + base
        lane = lax.broadcasted_iota(jnp.int32, pan.shape, 1)
        pan = jnp.where((lane < k) & (lane < sub), 0.0, pan)
        b_ref[base:end, :] = pan
        if end < k:
            part = jnp.where((lane >= end) & (lane < k), pan, 0.0)[:, :kp]
            upd = lax.dot_general(
                part, pan, (((0,), (0,)), ((), ())), precision=HIGHEST,
                preferred_element_type=jnp.float32,
            )
            b_ref[end:, :] = b_ref[end:, :] - upd[end:k]
    u_ref[...] = b_ref[:, :k]
    rest = b_ref[:, k:]
    parts = []
    for _ in range(3):
        term = rest.astype(jnp.bfloat16)
        parts.append(term)
        rest = rest - term.astype(jnp.float32)
    dims = (((1,), (1,)), ((), ()))
    for y_ref, o_ref in ((ys_ref, bs_ref), (yr_ref, br_ref)):
        n = y_ref.shape[0]
        step = 512 if n % 512 == 0 else n
        for i in range(0, n, step):
            y = y_ref[i : i + step, :]
            acc = None
            for part in parts:
                t = lax.dot_general(y, part, dims, preferred_element_type=jnp.float32)
                acc = t if acc is None else acc + t
            o_ref[i : i + step, :] = acc.astype(o_ref.dtype)


def factor_and_basis(g, y_stat, y_rot):
    k = g.shape[0]
    panel = next((p for p in (96, 64, 48, 32, 16, 8) if k % p == 0), None)
    if panel is None:
        lower = jnp.linalg.cholesky(g)
        eye = jnp.eye(k, dtype=jnp.float32)
        inverse = lax.linalg.triangular_solve(lower, eye, left_side=True, lower=True)
        basis = [
            jnp.dot(y.astype(jnp.float32), inverse.T, precision=HIGHEST).astype(jnp.bfloat16)
            for y in (y_stat, y_rot)
        ]
        return lower.T, basis[0], basis[1]
    vmem = pl.BlockSpec(memory_space=pltpu.VMEM)
    return pl.pallas_call(
        functools.partial(_chol_kernel, panel=panel),
        out_shape=(
            jax.ShapeDtypeStruct((k, k), jnp.float32),
            jax.ShapeDtypeStruct(y_stat.shape, jnp.bfloat16),
            jax.ShapeDtypeStruct(y_rot.shape, jnp.bfloat16),
        ),
        in_specs=[vmem, vmem, vmem],
        out_specs=(vmem, vmem, vmem),
        scratch_shapes=[pltpu.VMEM((k, 2 * k), jnp.float32)],
    )(g, y_stat, y_rot)


def per_device(stationary, rotor_rows, owners, counts, omega):
    n_rows = lax.axis_size("rows")
    n_grp = lax.axis_size("grp")
    rot_dev = rotor_rows.shape[0]
    stat_dev = stationary.shape[0]
    total = n_grp * n_rows * (stat_dev + rot_dev)
    k = omega.shape[1]
    targets = owners[:, 0]
    live = lax.iota(jnp.int32, rot_dev) < counts[0]
    onehot = ((targets[:, None] == lax.iota(jnp.int32, n_rows)[None, :]) & live[:, None]).astype(
        jnp.int32
    )
    rank = jnp.sum((jnp.cumsum(onehot, axis=0) - onehot) * onehot, axis=1)
    slot = jnp.where(live, targets * CAP + rank, -1)
    select = (lax.iota(jnp.int32, n_rows * CAP)[:, None] == slot[None, :]).astype(jnp.bfloat16)

    sketch_stat = sketch_block(stationary, omega)
    sketch_rot = sketch_block(rotor_rows, omega)
    rot_live = jnp.where(live[:, None], sketch_rot, jnp.zeros_like(sketch_rot))

    dims = (((0,), (0,)), ((), ()))
    gram = lax.dot_general(sketch_stat, sketch_stat, dims, preferred_element_type=jnp.float32)
    gram = gram + lax.dot_general(rot_live, rot_live, dims, preferred_element_type=jnp.float32)
    gram = gram / total

    outgoing = jnp.dot(select, sketch_rot, preferred_element_type=jnp.float32).astype(jnp.bfloat16)
    outgoing = outgoing.reshape(n_rows, CAP, -1)
    packed = pack_sym(gram)
    n = n_grp * n_rows
    if n & (n - 1) or n_rows & (n_rows - 1) or (CAP * k) % packed.shape[1]:
        arrived = lax.all_to_all(outgoing, "rows", split_axis=0, concat_axis=0, tiled=True)
        packed = lax.psum(packed, AXES)
    else:
        packed, arrived = all_sum_and_route(packed, outgoing, n, n_rows)
    arrived = arrived.reshape(n_rows * CAP, -1)
    gram = unpack_sym(packed)
    upper, basis_stat, basis_rot = factor_and_basis(gram, sketch_stat, arrived)
    return (basis_stat, basis_rot, upper)


def solution(mesh):
    return jax.shard_map(
        per_device,
        mesh=mesh,
        in_specs=(
            P(("grp", "rows"), None),
            P(("grp", "rows"), None),
            P(("grp", "rows"), None),
            P(("grp", "rows")),
            P(),
        ),
        out_specs=(P(("grp", "rows"), None), P(("grp", "rows"), None), P()),
        check_vma=False,
    )
```

```python
import functools

import jax
import jax.numpy as jnp
from jax import lax
from jax.experimental import pallas as pl
from jax.experimental.pallas import tpu as pltpu
from jax.sharding import PartitionSpec as P

CAP = 6
AXES = ("grp", "rows")
HIGHEST = lax.Precision.HIGHEST
GROUP = 8


def sketch_block(block, omega):
    return jnp.dot(block, omega, preferred_element_type=jnp.float32).astype(jnp.bfloat16)


def pack_sym(g):
    h = g.shape[0] // 2
    i = lax.broadcasted_iota(jnp.int32, (h, h), 0)
    j = lax.broadcasted_iota(jnp.int32, (h, h), 1)
    a, b, c = g[:h, :h], g[h:, :h], g[h:, h:]
    m = jnp.where(i >= j, a, c)
    diag_c = jnp.sum(jnp.where(i == j, c, 0.0), axis=0, keepdims=True)
    return jnp.concatenate([b, m, diag_c], axis=0)


def unpack_sym(p):
    h = p.shape[1]
    b, m, diag_c = p[:h], p[h : 2 * h], p[2 * h :]
    i = lax.broadcasted_iota(jnp.int32, (h, h), 0)
    j = lax.broadcasted_iota(jnp.int32, (h, h), 1)
    mt = m.T
    a = jnp.where(i >= j, m, mt)
    c = jnp.where(i < j, m, jnp.where(i > j, mt, diag_c))
    return jnp.concatenate(
        [jnp.concatenate([a, b.T], axis=1), jnp.concatenate([b, c], axis=1)], axis=0
    )


def all_sum_and_route(x, held, n, n_rows):
    bits = n.bit_length() - 1
    row_bits = n_rows.bit_length() - 1
    me = lax.axis_index(AXES)
    width = x.shape[1]
    for b in reversed(range(bits)):
        perm = [(i, i ^ (1 << b)) for i in range(n)]
        if b >= row_bits:
            x = x + lax.ppermute(x, AXES, perm)
            continue
        parts = held.reshape((n_rows >> (b + 1), 2, 1 << b) + held.shape[1:])
        mine = (me >> b) & 1
        keep = jnp.where(mine == 0, parts[:, 0], parts[:, 1])
        away = jnp.where(mine == 0, parts[:, 1], parts[:, 0])
        packet = jnp.concatenate([x, away.astype(jnp.float32).reshape(-1, width)], axis=0)
        got = lax.ppermute(packet, AXES, perm)
        x = x + got[: x.shape[0]]
        came = got[x.shape[0] :].reshape(away.shape).astype(held.dtype)
        lo = jnp.where(mine == 0, keep, came)
        hi = jnp.where(mine == 0, came, keep)
        held = jnp.stack([lo, hi], axis=1).reshape(held.shape)
    return x, held


def _chol_kernel(g_ref, ys_ref, yr_ref, u_ref, bs_ref, br_ref, b_ref, *, panel):
    k = g_ref.shape[0]
    w = 2 * k
    kp = ((k + 127) // 128) * 128
    rows = lax.broadcasted_iota(jnp.int32, (k, k), 0)
    cols = lax.broadcasted_iota(jnp.int32, (k, k), 1)
    b_ref[:, :k] = g_ref[...]
    b_ref[:, k:] = jnp.where(rows == cols, 1.0, 0.0).astype(jnp.float32)
    for p in range(k // panel):
        base = p * panel
        end = base + panel
        pan = b_ref[base:end, :]
        for r in range(0, panel, GROUP):
            piv = base + r
            t0 = (piv // 128) * 128
            top, low = pan[:r], pan[r:]
            m = panel - r
            lane = lax.broadcasted_iota(jnp.int32, (m, 128), 1) + t0
            blk = low[:, t0 : t0 + 128]
            cs = [
                jnp.sum(jnp.where(lane == piv + t, blk, 0.0), axis=1, keepdims=True)
                for t in range(GROUP)
            ]
            coefs, vs = [], []
            for t in range(GROUP):
                c, row = cs[t], low[t : t + 1]
                for u in range(t):
                    lu = coefs[u][t : t + 1]
                    c = c - coefs[u] * lu
                    row = row - lu * vs[u]
                s = lax.rsqrt(c[t : t + 1])
                vs.append(row * s)
                coefs.append(c * s)
            sub = lax.broadcasted_iota(jnp.int32, (m, w), 0)
            upd = low
            for t in range(GROUP):
                upd = upd - coefs[t] * vs[t]
            low = jnp.where(sub >= GROUP, upd, low)
            for t in range(GROUP):
                low = jnp.where(sub == t, vs[t], low)
            pan = jnp.concatenate([top, low], axis=0) if r else low
        sub = lax.broadcasted_iota(jnp.int32, pan.shape, 0) + base
        lane = lax.broadcasted_iota(jnp.int32, pan.shape, 1)
        pan = jnp.where((lane < k) & (lane < sub), 0.0, pan)
        b_ref[base:end, :] = pan
        if end < k:
            part = jnp.where((lane >= end) & (lane < k), pan, 0.0)[:, :kp]
            upd = lax.dot_general(
                part, pan, (((0,), (0,)), ((), ())), precision=HIGHEST,
                preferred_element_type=jnp.float32,
            )
            b_ref[end:, :] = b_ref[end:, :] - upd[end:k]
    u_ref[...] = b_ref[:, :k]
    rest = b_ref[:, k:]
    parts = []
    for _ in range(3):
        term = rest.astype(jnp.bfloat16)
        parts.append(term)
        rest = rest - term.astype(jnp.float32)
    dims = (((1,), (1,)), ((), ()))
    for y_ref, o_ref, flip in ((ys_ref, bs_ref, True), (yr_ref, br_ref, False)):
        n = y_ref.shape[0]
        step = 512 if n % 512 == 0 else n
        for i in range(0, n, step):
            y = y_ref[i : i + step, :]
            acc = None
            for part in parts:
                pair = (part, y) if flip else (y, part)
                t = lax.dot_general(*pair, dims, preferred_element_type=jnp.float32)
                acc = t if acc is None else acc + t
            if flip:
                o_ref[:, i : i + step] = acc.astype(o_ref.dtype)
            else:
                o_ref[i : i + step, :] = acc.astype(o_ref.dtype)


def factor_and_basis(g, y_stat, y_rot):
    k = g.shape[0]
    panel = next((p for p in (96, 64, 48, 32, 16, 8) if k % p == 0), None)
    if panel is None:
        lower = jnp.linalg.cholesky(g)
        eye = jnp.eye(k, dtype=jnp.float32)
        inverse = lax.linalg.triangular_solve(lower, eye, left_side=True, lower=True)
        basis = [
            jnp.dot(y.astype(jnp.float32), inverse.T, precision=HIGHEST).astype(jnp.bfloat16)
            for y in (y_stat, y_rot)
        ]
        return lower.T, basis[0], basis[1]
    vmem = pl.BlockSpec(memory_space=pltpu.VMEM)
    upper, basis_stat_t, basis_rot = pl.pallas_call(
        functools.partial(_chol_kernel, panel=panel),
        out_shape=(
            jax.ShapeDtypeStruct((k, k), jnp.float32),
            jax.ShapeDtypeStruct(y_stat.shape[::-1], jnp.bfloat16),
            jax.ShapeDtypeStruct(y_rot.shape, jnp.bfloat16),
        ),
        in_specs=[vmem, vmem, vmem],
        out_specs=(vmem, vmem, vmem),
        scratch_shapes=[pltpu.VMEM((k, 2 * k), jnp.float32)],
    )(g, y_stat, y_rot)
    return upper, basis_stat_t.T, basis_rot


def per_device(stationary, rotor_rows, owners, counts, omega):
    n_rows = lax.axis_size("rows")
    n_grp = lax.axis_size("grp")
    rot_dev = rotor_rows.shape[0]
    stat_dev = stationary.shape[0]
    total = n_grp * n_rows * (stat_dev + rot_dev)
    k = omega.shape[1]
    targets = owners[:, 0]
    live = lax.iota(jnp.int32, rot_dev) < counts[0]
    onehot = ((targets[:, None] == lax.iota(jnp.int32, n_rows)[None, :]) & live[:, None]).astype(
        jnp.int32
    )
    rank = jnp.sum((jnp.cumsum(onehot, axis=0) - onehot) * onehot, axis=1)
    slot = jnp.where(live, targets * CAP + rank, -1)
    select = (lax.iota(jnp.int32, n_rows * CAP)[:, None] == slot[None, :]).astype(jnp.bfloat16)

    sketch_stat = sketch_block(stationary, omega)
    sketch_rot = sketch_block(rotor_rows, omega)
    rot_live = jnp.where(live[:, None], sketch_rot, jnp.zeros_like(sketch_rot))

    dims = (((0,), (0,)), ((), ()))
    gram = lax.dot_general(sketch_stat, sketch_stat, dims, preferred_element_type=jnp.float32)
    gram = gram + lax.dot_general(rot_live, rot_live, dims, preferred_element_type=jnp.float32)
    gram = gram / total

    outgoing = jnp.dot(select, sketch_rot, preferred_element_type=jnp.float32).astype(jnp.bfloat16)
    outgoing = outgoing.reshape(n_rows, CAP, -1)
    packed = pack_sym(gram)
    n = n_grp * n_rows
    if n & (n - 1) or n_rows & (n_rows - 1) or (CAP * k) % packed.shape[1]:
        arrived = lax.all_to_all(outgoing, "rows", split_axis=0, concat_axis=0, tiled=True)
        packed = lax.psum(packed, AXES)
    else:
        packed, arrived = all_sum_and_route(packed, outgoing, n, n_rows)
    arrived = arrived.reshape(n_rows * CAP, -1)
    gram = unpack_sym(packed)
    upper, basis_stat, basis_rot = factor_and_basis(gram, sketch_stat, arrived)
    return (basis_stat, basis_rot, upper)


def solution(mesh):
    return jax.shard_map(
        per_device,
        mesh=mesh,
        in_specs=(
            P(("grp", "rows"), None),
            P(("grp", "rows"), None),
            P(("grp", "rows"), None),
            P(("grp", "rows")),
            P(),
        ),
        out_specs=(P(("grp", "rows"), None), P(("grp", "rows"), None), P()),
        check_vma=False,
    )
```

```python
import functools

import jax
import jax.numpy as jnp
from jax import lax
from jax.experimental import pallas as pl
from jax.experimental.pallas import tpu as pltpu
from jax.sharding import PartitionSpec as P

CAP = 6
AXES = ("grp", "rows")
HIGHEST = lax.Precision.HIGHEST
GROUP = 16


def sketch_block(block, omega):
    return jnp.dot(block, omega, preferred_element_type=jnp.float32).astype(jnp.bfloat16)


def pack_sym(g):
    h = g.shape[0] // 2
    i = lax.broadcasted_iota(jnp.int32, (h, h), 0)
    j = lax.broadcasted_iota(jnp.int32, (h, h), 1)
    a, b, c = g[:h, :h], g[h:, :h], g[h:, h:]
    m = jnp.where(i >= j, a, c)
    diag_c = jnp.sum(jnp.where(i == j, c, 0.0), axis=0, keepdims=True)
    return jnp.concatenate([b, m, diag_c], axis=0)


def unpack_sym(p):
    h = p.shape[1]
    b, m, diag_c = p[:h], p[h : 2 * h], p[2 * h :]
    i = lax.broadcasted_iota(jnp.int32, (h, h), 0)
    j = lax.broadcasted_iota(jnp.int32, (h, h), 1)
    mt = m.T
    a = jnp.where(i >= j, m, mt)
    c = jnp.where(i < j, m, jnp.where(i > j, mt, diag_c))
    return jnp.concatenate(
        [jnp.concatenate([a, b.T], axis=1), jnp.concatenate([b, c], axis=1)], axis=0
    )


def all_sum_and_route(x, held, n, n_rows):
    bits = n.bit_length() - 1
    row_bits = n_rows.bit_length() - 1
    me = lax.axis_index(AXES)
    width = x.shape[1]
    for b in reversed(range(bits)):
        perm = [(i, i ^ (1 << b)) for i in range(n)]
        if b >= row_bits:
            x = x + lax.ppermute(x, AXES, perm)
            continue
        parts = held.reshape((n_rows >> (b + 1), 2, 1 << b) + held.shape[1:])
        mine = (me >> b) & 1
        keep = jnp.where(mine == 0, parts[:, 0], parts[:, 1])
        away = jnp.where(mine == 0, parts[:, 1], parts[:, 0])
        packet = jnp.concatenate([x, away.astype(jnp.float32).reshape(-1, width)], axis=0)
        got = lax.ppermute(packet, AXES, perm)
        x = x + got[: x.shape[0]]
        came = got[x.shape[0] :].reshape(away.shape).astype(held.dtype)
        lo = jnp.where(mine == 0, keep, came)
        hi = jnp.where(mine == 0, came, keep)
        held = jnp.stack([lo, hi], axis=1).reshape(held.shape)
    return x, held


def _chol_kernel(g_ref, ys_ref, yr_ref, u_ref, bs_ref, br_ref, b_ref, *, panel):
    k = g_ref.shape[0]
    w = 2 * k
    kp = ((k + 127) // 128) * 128
    rows = lax.broadcasted_iota(jnp.int32, (k, k), 0)
    cols = lax.broadcasted_iota(jnp.int32, (k, k), 1)
    b_ref[:, :k] = g_ref[...]
    b_ref[:, k:] = jnp.where(rows == cols, 1.0, 0.0).astype(jnp.float32)
    for p in range(k // panel):
        base = p * panel
        end = base + panel
        pan = b_ref[base:end, :]
        for r in range(0, panel, GROUP):
            piv = base + r
            t0 = (piv // 128) * 128
            top, low = pan[:r], pan[r:]
            m = panel - r
            lane = lax.broadcasted_iota(jnp.int32, (m, 128), 1) + t0
            blk = low[:, t0 : t0 + 128]
            cs = [
                jnp.sum(jnp.where(lane == piv + t, blk, 0.0), axis=1, keepdims=True)
                for t in range(GROUP)
            ]
            coefs, vs = [], []
            for t in range(GROUP):
                c, row = cs[t], low[t : t + 1]
                for u in range(t):
                    lu = coefs[u][t : t + 1]
                    c = c - coefs[u] * lu
                    row = row - lu * vs[u]
                s = lax.rsqrt(c[t : t + 1])
                vs.append(row * s)
                coefs.append(c * s)
            sub = lax.broadcasted_iota(jnp.int32, (m, w), 0)
            upd = low
            for t in range(GROUP):
                upd = upd - coefs[t] * vs[t]
            low = jnp.where(sub >= GROUP, upd, low)
            for t in range(GROUP):
                low = jnp.where(sub == t, vs[t], low)
            pan = jnp.concatenate([top, low], axis=0) if r else low
        sub = lax.broadcasted_iota(jnp.int32, pan.shape, 0) + base
        lane = lax.broadcasted_iota(jnp.int32, pan.shape, 1)
        pan = jnp.where((lane < k) & (lane < sub), 0.0, pan)
        b_ref[base:end, :] = pan
        if end < k:
            part = jnp.where((lane >= end) & (lane < k), pan, 0.0)[:, :kp]
            upd = lax.dot_general(
                part, pan, (((0,), (0,)), ((), ())), precision=HIGHEST,
                preferred_element_type=jnp.float32,
            )
            b_ref[end:, :] = b_ref[end:, :] - upd[end:k]
    u_ref[...] = b_ref[:, :k]
    rest = b_ref[:, k:]
    parts = []
    for _ in range(3):
        term = rest.astype(jnp.bfloat16)
        parts.append(term)
        rest = rest - term.astype(jnp.float32)
    dims = (((1,), (1,)), ((), ()))
    for y_ref, o_ref, flip in ((ys_ref, bs_ref, True), (yr_ref, br_ref, False)):
        n = y_ref.shape[0]
        step = 512 if n % 512 == 0 else n
        for i in range(0, n, step):
            y = y_ref[i : i + step, :]
            acc = None
            for part in parts:
                pair = (part, y) if flip else (y, part)
                t = lax.dot_general(*pair, dims, preferred_element_type=jnp.float32)
                acc = t if acc is None else acc + t
            if flip:
                o_ref[:, i : i + step] = acc.astype(o_ref.dtype)
            else:
                o_ref[i : i + step, :] = acc.astype(o_ref.dtype)


def factor_and_basis(g, y_stat, y_rot):
    k = g.shape[0]
    panel = next((p for p in (96, 64, 48, 32, 16) if k % p == 0 and p % GROUP == 0), None)
    if panel is None:
        lower = jnp.linalg.cholesky(g)
        eye = jnp.eye(k, dtype=jnp.float32)
        inverse = lax.linalg.triangular_solve(lower, eye, left_side=True, lower=True)
        basis = [
            jnp.dot(y.astype(jnp.float32), inverse.T, precision=HIGHEST).astype(jnp.bfloat16)
            for y in (y_stat, y_rot)
        ]
        return lower.T, basis[0], basis[1]
    vmem = pl.BlockSpec(memory_space=pltpu.VMEM)
    upper, basis_stat_t, basis_rot = pl.pallas_call(
        functools.partial(_chol_kernel, panel=panel),
        out_shape=(
            jax.ShapeDtypeStruct((k, k), jnp.float32),
            jax.ShapeDtypeStruct(y_stat.shape[::-1], jnp.bfloat16),
            jax.ShapeDtypeStruct(y_rot.shape, jnp.bfloat16),
        ),
        in_specs=[vmem, vmem, vmem],
        out_specs=(vmem, vmem, vmem),
        scratch_shapes=[pltpu.VMEM((k, 2 * k), jnp.float32)],
    )(g, y_stat, y_rot)
    return upper, basis_stat_t.T, basis_rot


def per_device(stationary, rotor_rows, owners, counts, omega):
    n_rows = lax.axis_size("rows")
    n_grp = lax.axis_size("grp")
    rot_dev = rotor_rows.shape[0]
    stat_dev = stationary.shape[0]
    total = n_grp * n_rows * (stat_dev + rot_dev)
    k = omega.shape[1]
    targets = owners[:, 0]
    live = lax.iota(jnp.int32, rot_dev) < counts[0]
    onehot = ((targets[:, None] == lax.iota(jnp.int32, n_rows)[None, :]) & live[:, None]).astype(
        jnp.int32
    )
    rank = jnp.sum((jnp.cumsum(onehot, axis=0) - onehot) * onehot, axis=1)
    slot = jnp.where(live, targets * CAP + rank, -1)
    select = (lax.iota(jnp.int32, n_rows * CAP)[:, None] == slot[None, :]).astype(jnp.bfloat16)

    sketch_stat = sketch_block(stationary, omega)
    sketch_rot = sketch_block(rotor_rows, omega)
    rot_live = jnp.where(live[:, None], sketch_rot, jnp.zeros_like(sketch_rot))

    dims = (((0,), (0,)), ((), ()))
    gram = lax.dot_general(sketch_stat, sketch_stat, dims, preferred_element_type=jnp.float32)
    gram = gram + lax.dot_general(rot_live, rot_live, dims, preferred_element_type=jnp.float32)
    gram = gram / total

    outgoing = jnp.dot(select, sketch_rot, preferred_element_type=jnp.float32).astype(jnp.bfloat16)
    outgoing = outgoing.reshape(n_rows, CAP, -1)
    packed = pack_sym(gram)
    n = n_grp * n_rows
    if n & (n - 1) or n_rows & (n_rows - 1) or (CAP * k) % packed.shape[1]:
        arrived = lax.all_to_all(outgoing, "rows", split_axis=0, concat_axis=0, tiled=True)
        packed = lax.psum(packed, AXES)
    else:
        packed, arrived = all_sum_and_route(packed, outgoing, n, n_rows)
    arrived = arrived.reshape(n_rows * CAP, -1)
    gram = unpack_sym(packed)
    upper, basis_stat, basis_rot = factor_and_basis(gram, sketch_stat, arrived)
    return (basis_stat, basis_rot, upper)


def solution(mesh):
    return jax.shard_map(
        per_device,
        mesh=mesh,
        in_specs=(
            P(("grp", "rows"), None),
            P(("grp", "rows"), None),
            P(("grp", "rows"), None),
            P(("grp", "rows")),
            P(),
        ),
        out_specs=(P(("grp", "rows"), None), P(("grp", "rows"), None), P()),
        check_vma=False,
    )
```

```python
import functools

import jax
import jax.numpy as jnp
from jax import lax
from jax.experimental import pallas as pl
from jax.experimental.pallas import tpu as pltpu
from jax.sharding import PartitionSpec as P

CAP = 6
AXES = ("grp", "rows")
HIGHEST = lax.Precision.HIGHEST
GROUP = 8


def sketch_block(block, omega):
    return jnp.dot(block, omega, preferred_element_type=jnp.float32).astype(jnp.bfloat16)


def _sketch_kernel(x_ref, w_ref, s_ref, g_ref):
    @pl.when(pl.program_id(0) == 0)
    def _():
        g_ref[...] = jnp.zeros_like(g_ref)

    s = jnp.dot(x_ref[...], w_ref[...], preferred_element_type=jnp.float32).astype(jnp.bfloat16)
    s_ref[...] = s
    g_ref[...] += lax.dot_general(
        s, s, (((0,), (0,)), ((), ())), preferred_element_type=jnp.float32
    )


def sketch_and_gram(x, w):
    n, k = x.shape[0], w.shape[1]
    step = next((c for c in (512, 256, 128, 64, 32, 16) if n % c == 0), None)
    if step is None:
        s = sketch_block(x, w)
        dims = (((0,), (0,)), ((), ()))
        return s, lax.dot_general(s, s, dims, preferred_element_type=jnp.float32)
    return pl.pallas_call(
        _sketch_kernel,
        grid=(n // step,),
        in_specs=[
            pl.BlockSpec((step, x.shape[1]), lambda i: (i, 0)),
            pl.BlockSpec(w.shape, lambda i: (0, 0)),
        ],
        out_specs=(
            pl.BlockSpec((step, k), lambda i: (i, 0)),
            pl.BlockSpec((k, k), lambda i: (0, 0)),
        ),
        out_shape=(
            jax.ShapeDtypeStruct((n, k), jnp.bfloat16),
            jax.ShapeDtypeStruct((k, k), jnp.float32),
        ),
        compiler_params=pltpu.CompilerParams(dimension_semantics=("arbitrary",)),
    )(x, w)


def pack_sym(g):
    h = g.shape[0] // 2
    i = lax.broadcasted_iota(jnp.int32, (h, h), 0)
    j = lax.broadcasted_iota(jnp.int32, (h, h), 1)
    a, b, c = g[:h, :h], g[h:, :h], g[h:, h:]
    m = jnp.where(i >= j, a, c)
    diag_c = jnp.sum(jnp.where(i == j, c, 0.0), axis=0, keepdims=True)
    return jnp.concatenate([b, m, diag_c], axis=0)


def unpack_sym(p):
    h = p.shape[1]
    b, m, diag_c = p[:h], p[h : 2 * h], p[2 * h :]
    i = lax.broadcasted_iota(jnp.int32, (h, h), 0)
    j = lax.broadcasted_iota(jnp.int32, (h, h), 1)
    mt = m.T
    a = jnp.where(i >= j, m, mt)
    c = jnp.where(i < j, m, jnp.where(i > j, mt, diag_c))
    return jnp.concatenate(
        [jnp.concatenate([a, b.T], axis=1), jnp.concatenate([b, c], axis=1)], axis=0
    )


def all_sum_and_route(x, held, n, n_rows):
    bits = n.bit_length() - 1
    row_bits = n_rows.bit_length() - 1
    me = lax.axis_index(AXES)
    width = x.shape[1]
    for b in reversed(range(bits)):
        perm = [(i, i ^ (1 << b)) for i in range(n)]
        if b >= row_bits:
            x = x + lax.ppermute(x, AXES, perm)
            continue
        parts = held.reshape((n_rows >> (b + 1), 2, 1 << b) + held.shape[1:])
        mine = (me >> b) & 1
        keep = jnp.where(mine == 0, parts[:, 0], parts[:, 1])
        away = jnp.where(mine == 0, parts[:, 1], parts[:, 0])
        packet = jnp.concatenate([x, away.astype(jnp.float32).reshape(-1, width)], axis=0)
        got = lax.ppermute(packet, AXES, perm)
        x = x + got[: x.shape[0]]
        came = got[x.shape[0] :].reshape(away.shape).astype(held.dtype)
        lo = jnp.where(mine == 0, keep, came)
        hi = jnp.where(mine == 0, came, keep)
        held = jnp.stack([lo, hi], axis=1).reshape(held.shape)
    return x, held


def _chol_kernel(g_ref, ys_ref, yr_ref, u_ref, bs_ref, br_ref, b_ref, *, panel):
    k = g_ref.shape[0]
    w = 2 * k
    kp = ((k + 127) // 128) * 128
    rows = lax.broadcasted_iota(jnp.int32, (k, k), 0)
    cols = lax.broadcasted_iota(jnp.int32, (k, k), 1)
    b_ref[:, :k] = g_ref[...]
    b_ref[:, k:] = jnp.where(rows == cols, 1.0, 0.0).astype(jnp.float32)
    for p in range(k // panel):
        base = p * panel
        end = base + panel
        pan = b_ref[base:end, :]
        for r in range(0, panel, GROUP):
            piv = base + r
            t0 = (piv // 128) * 128
            top, low = pan[:r], pan[r:]
            m = panel - r
            lane = lax.broadcasted_iota(jnp.int32, (m, 128), 1) + t0
            blk = low[:, t0 : t0 + 128]
            cs = [
                jnp.sum(jnp.where(lane == piv + t, blk, 0.0), axis=1, keepdims=True)
                for t in range(GROUP)
            ]
            coefs, vs = [], []
            for t in range(GROUP):
                c, row = cs[t], low[t : t + 1]
                for u in range(t):
                    lu = coefs[u][t : t + 1]
                    c = c - coefs[u] * lu
                    row = row - lu * vs[u]
                s = lax.rsqrt(c[t : t + 1])
                vs.append(row * s)
                coefs.append(c * s)
            sub = lax.broadcasted_iota(jnp.int32, (m, w), 0)
            upd = low
            for t in range(GROUP):
                upd = upd - coefs[t] * vs[t]
            low = jnp.where(sub >= GROUP, upd, low)
            for t in range(GROUP):
                low = jnp.where(sub == t, vs[t], low)
            pan = jnp.concatenate([top, low], axis=0) if r else low
        sub = lax.broadcasted_iota(jnp.int32, pan.shape, 0) + base
        lane = lax.broadcasted_iota(jnp.int32, pan.shape, 1)
        pan = jnp.where((lane < k) & (lane < sub), 0.0, pan)
        b_ref[base:end, :] = pan
        if end < k:
            part = jnp.where((lane >= end) & (lane < k), pan, 0.0)[:, :kp]
            upd = lax.dot_general(
                part, pan, (((0,), (0,)), ((), ())), precision=HIGHEST,
                preferred_element_type=jnp.float32,
            )
            b_ref[end:, :] = b_ref[end:, :] - upd[end:k]
    u_ref[...] = b_ref[:, :k]
    rest = b_ref[:, k:]
    parts = []
    for _ in range(3):
        term = rest.astype(jnp.bfloat16)
        parts.append(term)
        rest = rest - term.astype(jnp.float32)
    dims = (((1,), (1,)), ((), ()))
    for y_ref, o_ref, flip in ((ys_ref, bs_ref, True), (yr_ref, br_ref, False)):
        n = y_ref.shape[0]
        step = 512 if n % 512 == 0 else n
        for i in range(0, n, step):
            y = y_ref[i : i + step, :]
            acc = None
            for part in parts:
                pair = (part, y) if flip else (y, part)
                t = lax.dot_general(*pair, dims, preferred_element_type=jnp.float32)
                acc = t if acc is None else acc + t
            if flip:
                o_ref[:, i : i + step] = acc.astype(o_ref.dtype)
            else:
                o_ref[i : i + step, :] = acc.astype(o_ref.dtype)


def factor_and_basis(g, y_stat, y_rot):
    k = g.shape[0]
    panel = next((p for p in (96, 64, 48, 32, 16, 8) if k % p == 0), None)
    if panel is None:
        lower = jnp.linalg.cholesky(g)
        eye = jnp.eye(k, dtype=jnp.float32)
        inverse = lax.linalg.triangular_solve(lower, eye, left_side=True, lower=True)
        basis = [
            jnp.dot(y.astype(jnp.float32), inverse.T, precision=HIGHEST).astype(jnp.bfloat16)
            for y in (y_stat, y_rot)
        ]
        return lower.T, basis[0], basis[1]
    vmem = pl.BlockSpec(memory_space=pltpu.VMEM)
    upper, basis_stat_t, basis_rot = pl.pallas_call(
        functools.partial(_chol_kernel, panel=panel),
        out_shape=(
            jax.ShapeDtypeStruct((k, k), jnp.float32),
            jax.ShapeDtypeStruct(y_stat.shape[::-1], jnp.bfloat16),
            jax.ShapeDtypeStruct(y_rot.shape, jnp.bfloat16),
        ),
        in_specs=[vmem, vmem, vmem],
        out_specs=(vmem, vmem, vmem),
        scratch_shapes=[pltpu.VMEM((k, 2 * k), jnp.float32)],
    )(g, y_stat, y_rot)
    return upper, basis_stat_t.T, basis_rot


def per_device(stationary, rotor_rows, owners, counts, omega):
    n_rows = lax.axis_size("rows")
    n_grp = lax.axis_size("grp")
    rot_dev = rotor_rows.shape[0]
    stat_dev = stationary.shape[0]
    total = n_grp * n_rows * (stat_dev + rot_dev)
    k = omega.shape[1]
    targets = owners[:, 0]
    live = lax.iota(jnp.int32, rot_dev) < counts[0]
    onehot = ((targets[:, None] == lax.iota(jnp.int32, n_rows)[None, :]) & live[:, None]).astype(
        jnp.int32
    )
    rank = jnp.sum((jnp.cumsum(onehot, axis=0) - onehot) * onehot, axis=1)
    slot = jnp.where(live, targets * CAP + rank, -1)
    select = (lax.iota(jnp.int32, n_rows * CAP)[:, None] == slot[None, :]).astype(jnp.bfloat16)

    sketch_stat, gram_stat = sketch_and_gram(stationary, omega)
    sketch_rot = sketch_block(rotor_rows, omega)
    rot_live = jnp.where(live[:, None], sketch_rot, jnp.zeros_like(sketch_rot))

    dims = (((0,), (0,)), ((), ()))
    gram = gram_stat + lax.dot_general(rot_live, rot_live, dims, preferred_element_type=jnp.float32)
    gram = gram / total

    outgoing = jnp.dot(select, sketch_rot, preferred_element_type=jnp.float32).astype(jnp.bfloat16)
    outgoing = outgoing.reshape(n_rows, CAP, -1)
    packed = pack_sym(gram)
    n = n_grp * n_rows
    if n & (n - 1) or n_rows & (n_rows - 1) or (CAP * k) % packed.shape[1]:
        arrived = lax.all_to_all(outgoing, "rows", split_axis=0, concat_axis=0, tiled=True)
        packed = lax.psum(packed, AXES)
    else:
        packed, arrived = all_sum_and_route(packed, outgoing, n, n_rows)
    arrived = arrived.reshape(n_rows * CAP, -1)
    gram = unpack_sym(packed)
    upper, basis_stat, basis_rot = factor_and_basis(gram, sketch_stat, arrived)
    return (basis_stat, basis_rot, upper)


def solution(mesh):
    return jax.shard_map(
        per_device,
        mesh=mesh,
        in_specs=(
            P(("grp", "rows"), None),
            P(("grp", "rows"), None),
            P(("grp", "rows"), None),
            P(("grp", "rows")),
            P(),
        ),
        out_specs=(P(("grp", "rows"), None), P(("grp", "rows"), None), P()),
        check_vma=False,
    )
```

```python
import functools

import jax
import jax.numpy as jnp
from jax import lax
from jax.experimental import pallas as pl
from jax.experimental.pallas import tpu as pltpu
from jax.sharding import PartitionSpec as P

CAP = 6
AXES = ("grp", "rows")
HIGHEST = lax.Precision.HIGHEST
GROUP = 8


def sketch_block(block, omega):
    return jnp.dot(block, omega, preferred_element_type=jnp.float32).astype(jnp.bfloat16)


def pack_sym(g):
    h = g.shape[0] // 2
    i = lax.broadcasted_iota(jnp.int32, (h, h), 0)
    j = lax.broadcasted_iota(jnp.int32, (h, h), 1)
    a, b, c = g[:h, :h], g[h:, :h], g[h:, h:]
    m = jnp.where(i >= j, a, c)
    diag_c = jnp.sum(jnp.where(i == j, c, 0.0), axis=0, keepdims=True)
    return jnp.concatenate([b, m, diag_c], axis=0)


def unpack_sym(p):
    h = p.shape[1]
    b, m, diag_c = p[:h], p[h : 2 * h], p[2 * h :]
    i = lax.broadcasted_iota(jnp.int32, (h, h), 0)
    j = lax.broadcasted_iota(jnp.int32, (h, h), 1)
    mt = m.T
    a = jnp.where(i >= j, m, mt)
    c = jnp.where(i < j, m, jnp.where(i > j, mt, diag_c))
    return jnp.concatenate(
        [jnp.concatenate([a, b.T], axis=1), jnp.concatenate([b, c], axis=1)], axis=0
    )


def all_sum_and_route(x, held, n, n_rows):
    bits = n.bit_length() - 1
    row_bits = n_rows.bit_length() - 1
    me = lax.axis_index(AXES)
    width = x.shape[1]
    for b in reversed(range(bits)):
        perm = [(i, i ^ (1 << b)) for i in range(n)]
        if b >= row_bits:
            x = x + lax.ppermute(x, AXES, perm)
            continue
        parts = held.reshape((n_rows >> (b + 1), 2, 1 << b) + held.shape[1:])
        mine = (me >> b) & 1
        keep = jnp.where(mine == 0, parts[:, 0], parts[:, 1])
        away = jnp.where(mine == 0, parts[:, 1], parts[:, 0])
        packet = jnp.concatenate([x, away.astype(jnp.float32).reshape(-1, width)], axis=0)
        got = lax.ppermute(packet, AXES, perm)
        x = x + got[: x.shape[0]]
        came = got[x.shape[0] :].reshape(away.shape).astype(held.dtype)
        lo = jnp.where(mine == 0, keep, came)
        hi = jnp.where(mine == 0, came, keep)
        held = jnp.stack([lo, hi], axis=1).reshape(held.shape)
    return x, held


def _chol_kernel(g_ref, ys_ref, yr_ref, u_ref, bs_ref, br_ref, b_ref, *, panel):
    k = g_ref.shape[1] * 2
    w = 2 * k
    kp = ((k + 127) // 128) * 128
    rows = lax.broadcasted_iota(jnp.int32, (k, k), 0)
    cols = lax.broadcasted_iota(jnp.int32, (k, k), 1)
    h = k // 2
    packed = g_ref[...]
    lower_b, mixed, diag_c = packed[:h], packed[h : 2 * h], packed[2 * h : 2 * h + 1]
    i = lax.broadcasted_iota(jnp.int32, (h, h), 0)
    j = lax.broadcasted_iota(jnp.int32, (h, h), 1)
    mixed_t = mixed.T
    a = jnp.where(i >= j, mixed, mixed_t)
    c = jnp.where(i < j, mixed, jnp.where(i > j, mixed_t, diag_c))
    top = jnp.concatenate([a, lower_b.T], axis=1)
    b_ref[:, :k] = jnp.concatenate([top, jnp.concatenate([lower_b, c], axis=1)], axis=0)
    b_ref[:, k:] = jnp.where(rows == cols, 1.0, 0.0).astype(jnp.float32)
    for p in range(k // panel):
        base = p * panel
        end = base + panel
        pan = b_ref[base:end, :]
        for r in range(0, panel, GROUP):
            piv = base + r
            t0 = (piv // 128) * 128
            top, low = pan[:r], pan[r:]
            m = panel - r
            lane = lax.broadcasted_iota(jnp.int32, (m, 128), 1) + t0
            blk = low[:, t0 : t0 + 128]
            cs = [
                jnp.sum(jnp.where(lane == piv + t, blk, 0.0), axis=1, keepdims=True)
                for t in range(GROUP)
            ]
            coefs, vs = [], []
            for t in range(GROUP):
                c, row = cs[t], low[t : t + 1]
                for u in range(t):
                    lu = coefs[u][t : t + 1]
                    c = c - coefs[u] * lu
                    row = row - lu * vs[u]
                s = lax.rsqrt(c[t : t + 1])
                vs.append(row * s)
                coefs.append(c * s)
            sub = lax.broadcasted_iota(jnp.int32, (m, w), 0)
            upd = low
            for t in range(GROUP):
                upd = upd - coefs[t] * vs[t]
            low = jnp.where(sub >= GROUP, upd, low)
            for t in range(GROUP):
                low = jnp.where(sub == t, vs[t], low)
            pan = jnp.concatenate([top, low], axis=0) if r else low
        sub = lax.broadcasted_iota(jnp.int32, pan.shape, 0) + base
        lane = lax.broadcasted_iota(jnp.int32, pan.shape, 1)
        pan = jnp.where((lane < k) & (lane < sub), 0.0, pan)
        b_ref[base:end, :] = pan
        if end < k:
            part = jnp.where((lane >= end) & (lane < k), pan, 0.0)[:, :kp]
            upd = lax.dot_general(
                part, pan, (((0,), (0,)), ((), ())), precision=HIGHEST,
                preferred_element_type=jnp.float32,
            )
            b_ref[end:, :] = b_ref[end:, :] - upd[end:k]
    u_ref[...] = b_ref[:, :k]
    rest = b_ref[:, k:]
    parts = []
    for _ in range(3):
        term = rest.astype(jnp.bfloat16)
        parts.append(term)
        rest = rest - term.astype(jnp.float32)
    dims = (((1,), (1,)), ((), ()))
    for y_ref, o_ref, flip in ((ys_ref, bs_ref, True), (yr_ref, br_ref, False)):
        n = y_ref.shape[0]
        step = 512 if n % 512 == 0 else n
        for i in range(0, n, step):
            y = y_ref[i : i + step, :]
            acc = None
            for part in parts:
                pair = (part, y) if flip else (y, part)
                t = lax.dot_general(*pair, dims, preferred_element_type=jnp.float32)
                acc = t if acc is None else acc + t
            if flip:
                o_ref[:, i : i + step] = acc.astype(o_ref.dtype)
            else:
                o_ref[i : i + step, :] = acc.astype(o_ref.dtype)


def factor_and_basis(packed, y_stat, y_rot):
    k = packed.shape[1] * 2
    panel = next((p for p in (96, 64, 48, 32, 16, 8) if k % p == 0), None)
    if panel is None:
        lower = jnp.linalg.cholesky(unpack_sym(packed))
        eye = jnp.eye(k, dtype=jnp.float32)
        inverse = lax.linalg.triangular_solve(lower, eye, left_side=True, lower=True)
        basis = [
            jnp.dot(y.astype(jnp.float32), inverse.T, precision=HIGHEST).astype(jnp.bfloat16)
            for y in (y_stat, y_rot)
        ]
        return lower.T, basis[0], basis[1]
    vmem = pl.BlockSpec(memory_space=pltpu.VMEM)
    upper, basis_stat_t, basis_rot = pl.pallas_call(
        functools.partial(_chol_kernel, panel=panel),
        out_shape=(
            jax.ShapeDtypeStruct((k, k), jnp.float32),
            jax.ShapeDtypeStruct(y_stat.shape[::-1], jnp.bfloat16),
            jax.ShapeDtypeStruct(y_rot.shape, jnp.bfloat16),
        ),
        in_specs=[vmem, vmem, vmem],
        out_specs=(vmem, vmem, vmem),
        scratch_shapes=[pltpu.VMEM((k, 2 * k), jnp.float32)],
    )(packed, y_stat, y_rot)
    return upper, basis_stat_t.T, basis_rot


def per_device(stationary, rotor_rows, owners, counts, omega):
    n_rows = lax.axis_size("rows")
    n_grp = lax.axis_size("grp")
    rot_dev = rotor_rows.shape[0]
    stat_dev = stationary.shape[0]
    total = n_grp * n_rows * (stat_dev + rot_dev)
    k = omega.shape[1]
    targets = owners[:, 0]
    live = lax.iota(jnp.int32, rot_dev) < counts[0]
    onehot = ((targets[:, None] == lax.iota(jnp.int32, n_rows)[None, :]) & live[:, None]).astype(
        jnp.int32
    )
    rank = jnp.sum((jnp.cumsum(onehot, axis=0) - onehot) * onehot, axis=1)
    slot = jnp.where(live, targets * CAP + rank, -1)
    select = (lax.iota(jnp.int32, n_rows * CAP)[:, None] == slot[None, :]).astype(jnp.bfloat16)

    sketch_stat = sketch_block(stationary, omega)
    sketch_rot = sketch_block(rotor_rows, omega)
    rot_live = jnp.where(live[:, None], sketch_rot, jnp.zeros_like(sketch_rot))

    dims = (((0,), (0,)), ((), ()))
    gram = lax.dot_general(sketch_stat, sketch_stat, dims, preferred_element_type=jnp.float32)
    gram = gram + lax.dot_general(rot_live, rot_live, dims, preferred_element_type=jnp.float32)
    gram = gram / total

    outgoing = jnp.dot(select, sketch_rot, preferred_element_type=jnp.float32).astype(jnp.bfloat16)
    outgoing = outgoing.reshape(n_rows, CAP, -1)
    packed = pack_sym(gram)
    n = n_grp * n_rows
    if n & (n - 1) or n_rows & (n_rows - 1) or (CAP * k) % packed.shape[1]:
        arrived = lax.all_to_all(outgoing, "rows", split_axis=0, concat_axis=0, tiled=True)
        packed = lax.psum(packed, AXES)
    else:
        packed, arrived = all_sum_and_route(packed, outgoing, n, n_rows)
    arrived = arrived.reshape(n_rows * CAP, -1)
    upper, basis_stat, basis_rot = factor_and_basis(packed, sketch_stat, arrived)
    return (basis_stat, basis_rot, upper)


def solution(mesh):
    return jax.shard_map(
        per_device,
        mesh=mesh,
        in_specs=(
            P(("grp", "rows"), None),
            P(("grp", "rows"), None),
            P(("grp", "rows"), None),
            P(("grp", "rows")),
            P(),
        ),
        out_specs=(P(("grp", "rows"), None), P(("grp", "rows"), None), P()),
        check_vma=False,
    )
```

```python
import functools

import jax
import jax.numpy as jnp
from jax import lax
from jax.experimental import pallas as pl
from jax.experimental.pallas import tpu as pltpu
from jax.sharding import PartitionSpec as P

CAP = 6
AXES = ("grp", "rows")
HIGHEST = lax.Precision.HIGHEST
GROUP = 8


def sketch_block(block, omega):
    return jnp.dot(block, omega, preferred_element_type=jnp.float32).astype(jnp.bfloat16)


def pack_sym(g):
    h = g.shape[0] // 2
    i = lax.broadcasted_iota(jnp.int32, (h, h), 0)
    j = lax.broadcasted_iota(jnp.int32, (h, h), 1)
    a, b, c = g[:h, :h], g[h:, :h], g[h:, h:]
    m = jnp.where(i >= j, a, c)
    diag_c = jnp.sum(jnp.where(i == j, c, 0.0), axis=0, keepdims=True)
    return jnp.concatenate([b, m, diag_c], axis=0)


def unpack_sym(p):
    h = p.shape[1]
    b, m, diag_c = p[:h], p[h : 2 * h], p[2 * h :]
    i = lax.broadcasted_iota(jnp.int32, (h, h), 0)
    j = lax.broadcasted_iota(jnp.int32, (h, h), 1)
    mt = m.T
    a = jnp.where(i >= j, m, mt)
    c = jnp.where(i < j, m, jnp.where(i > j, mt, diag_c))
    return jnp.concatenate(
        [jnp.concatenate([a, b.T], axis=1), jnp.concatenate([b, c], axis=1)], axis=0
    )


def all_sum_and_route(x, held, n, n_rows):
    bits = n.bit_length() - 1
    row_bits = n_rows.bit_length() - 1
    me = lax.axis_index(AXES)
    width = x.shape[1]
    last = jnp.zeros_like(x)
    for b in reversed(range(bits)):
        perm = [(i, i ^ (1 << b)) for i in range(n)]
        if b >= row_bits:
            got = lax.ppermute(x, AXES, perm)
            if b == 0:
                last = got
            else:
                x = x + got
            continue
        parts = held.reshape((n_rows >> (b + 1), 2, 1 << b) + held.shape[1:])
        mine = (me >> b) & 1
        keep = jnp.where(mine == 0, parts[:, 0], parts[:, 1])
        away = jnp.where(mine == 0, parts[:, 1], parts[:, 0])
        packet = jnp.concatenate([x, away.astype(jnp.float32).reshape(-1, width)], axis=0)
        got = lax.ppermute(packet, AXES, perm)
        if b == 0:
            last = got[: x.shape[0]]
        else:
            x = x + got[: x.shape[0]]
        came = got[x.shape[0] :].reshape(away.shape).astype(held.dtype)
        lo = jnp.where(mine == 0, keep, came)
        hi = jnp.where(mine == 0, came, keep)
        held = jnp.stack([lo, hi], axis=1).reshape(held.shape)
    return (x, last), held


def _chol_kernel(g_ref, g2_ref, ys_ref, yr_ref, u_ref, bs_ref, br_ref, b_ref, *, panel):
    k = g_ref.shape[1] * 2
    w = 2 * k
    kp = ((k + 127) // 128) * 128
    rows = lax.broadcasted_iota(jnp.int32, (k, k), 0)
    cols = lax.broadcasted_iota(jnp.int32, (k, k), 1)
    h = k // 2
    packed = g_ref[...] + g2_ref[...]
    lower_b, mixed, diag_c = packed[:h], packed[h : 2 * h], packed[2 * h : 2 * h + 1]
    i = lax.broadcasted_iota(jnp.int32, (h, h), 0)
    j = lax.broadcasted_iota(jnp.int32, (h, h), 1)
    mixed_t = mixed.T
    a = jnp.where(i >= j, mixed, mixed_t)
    c = jnp.where(i < j, mixed, jnp.where(i > j, mixed_t, diag_c))
    top = jnp.concatenate([a, lower_b.T], axis=1)
    b_ref[:, :k] = jnp.concatenate([top, jnp.concatenate([lower_b, c], axis=1)], axis=0)
    b_ref[:, k:] = jnp.where(rows == cols, 1.0, 0.0).astype(jnp.float32)
    for p in range(k // panel):
        base = p * panel
        end = base + panel
        pan = b_ref[base:end, :]
        for r in range(0, panel, GROUP):
            piv = base + r
            t0 = (piv // 128) * 128
            top, low = pan[:r], pan[r:]
            m = panel - r
            lane = lax.broadcasted_iota(jnp.int32, (m, 128), 1) + t0
            blk = low[:, t0 : t0 + 128]
            cs = [
                jnp.sum(jnp.where(lane == piv + t, blk, 0.0), axis=1, keepdims=True)
                for t in range(GROUP)
            ]
            coefs, vs = [], []
            for t in range(GROUP):
                c, row = cs[t], low[t : t + 1]
                for u in range(t):
                    lu = coefs[u][t : t + 1]
                    c = c - coefs[u] * lu
                    row = row - lu * vs[u]
                s = lax.rsqrt(c[t : t + 1])
                vs.append(row * s)
                coefs.append(c * s)
            sub = lax.broadcasted_iota(jnp.int32, (m, w), 0)
            upd = low
            for t in range(GROUP):
                upd = upd - coefs[t] * vs[t]
            low = jnp.where(sub >= GROUP, upd, low)
            for t in range(GROUP):
                low = jnp.where(sub == t, vs[t], low)
            pan = jnp.concatenate([top, low], axis=0) if r else low
        sub = lax.broadcasted_iota(jnp.int32, pan.shape, 0) + base
        lane = lax.broadcasted_iota(jnp.int32, pan.shape, 1)
        pan = jnp.where((lane < k) & (lane < sub), 0.0, pan)
        b_ref[base:end, :] = pan
        if end < k:
            part = jnp.where((lane >= end) & (lane < k), pan, 0.0)[:, :kp]
            upd = lax.dot_general(
                part, pan, (((0,), (0,)), ((), ())), precision=HIGHEST,
                preferred_element_type=jnp.float32,
            )
            b_ref[end:, :] = b_ref[end:, :] - upd[end:k]
    u_ref[...] = b_ref[:, :k]
    rest = b_ref[:, k:]
    parts = []
    for _ in range(3):
        term = rest.astype(jnp.bfloat16)
        parts.append(term)
        rest = rest - term.astype(jnp.float32)
    dims = (((1,), (1,)), ((), ()))
    for y_ref, o_ref, flip in ((ys_ref, bs_ref, True), (yr_ref, br_ref, False)):
        n = y_ref.shape[0]
        step = 512 if n % 512 == 0 else n
        for i in range(0, n, step):
            y = y_ref[i : i + step, :]
            acc = None
            for part in parts:
                pair = (part, y) if flip else (y, part)
                t = lax.dot_general(*pair, dims, preferred_element_type=jnp.float32)
                acc = t if acc is None else acc + t
            if flip:
                o_ref[:, i : i + step] = acc.astype(o_ref.dtype)
            else:
                o_ref[i : i + step, :] = acc.astype(o_ref.dtype)


def factor_and_basis(packed, y_stat, y_rot):
    k = packed[0].shape[1] * 2
    panel = next((p for p in (96, 64, 48, 32, 16, 8) if k % p == 0), None)
    if panel is None:
        lower = jnp.linalg.cholesky(unpack_sym(packed[0] + packed[1]))
        eye = jnp.eye(k, dtype=jnp.float32)
        inverse = lax.linalg.triangular_solve(lower, eye, left_side=True, lower=True)
        basis = [
            jnp.dot(y.astype(jnp.float32), inverse.T, precision=HIGHEST).astype(jnp.bfloat16)
            for y in (y_stat, y_rot)
        ]
        return lower.T, basis[0], basis[1]
    vmem = pl.BlockSpec(memory_space=pltpu.VMEM)
    upper, basis_stat_t, basis_rot = pl.pallas_call(
        functools.partial(_chol_kernel, panel=panel),
        out_shape=(
            jax.ShapeDtypeStruct((k, k), jnp.float32),
            jax.ShapeDtypeStruct(y_stat.shape[::-1], jnp.bfloat16),
            jax.ShapeDtypeStruct(y_rot.shape, jnp.bfloat16),
        ),
        in_specs=[vmem, vmem, vmem, vmem],
        out_specs=(vmem, vmem, vmem),
        scratch_shapes=[pltpu.VMEM((k, 2 * k), jnp.float32)],
    )(*packed, y_stat, y_rot)
    return upper, basis_stat_t.T, basis_rot


def per_device(stationary, rotor_rows, owners, counts, omega):
    n_rows = lax.axis_size("rows")
    n_grp = lax.axis_size("grp")
    rot_dev = rotor_rows.shape[0]
    stat_dev = stationary.shape[0]
    total = n_grp * n_rows * (stat_dev + rot_dev)
    k = omega.shape[1]
    targets = owners[:, 0]
    live = lax.iota(jnp.int32, rot_dev) < counts[0]
    onehot = ((targets[:, None] == lax.iota(jnp.int32, n_rows)[None, :]) & live[:, None]).astype(
        jnp.int32
    )
    rank = jnp.sum((jnp.cumsum(onehot, axis=0) - onehot) * onehot, axis=1)
    slot = jnp.where(live, targets * CAP + rank, -1)
    select = (lax.iota(jnp.int32, n_rows * CAP)[:, None] == slot[None, :]).astype(jnp.bfloat16)

    sketch_stat = sketch_block(stationary, omega)
    sketch_rot = sketch_block(rotor_rows, omega)
    rot_live = jnp.where(live[:, None], sketch_rot, jnp.zeros_like(sketch_rot))

    dims = (((0,), (0,)), ((), ()))
    gram = lax.dot_general(sketch_stat, sketch_stat, dims, preferred_element_type=jnp.float32)
    gram = gram + lax.dot_general(rot_live, rot_live, dims, preferred_element_type=jnp.float32)
    gram = gram / total

    outgoing = jnp.dot(select, sketch_rot, preferred_element_type=jnp.float32).astype(jnp.bfloat16)
    outgoing = outgoing.reshape(n_rows, CAP, -1)
    packed = pack_sym(gram)
    n = n_grp * n_rows
    if n & (n - 1) or n_rows & (n_rows - 1) or (CAP * k) % packed.shape[1]:
        arrived = lax.all_to_all(outgoing, "rows", split_axis=0, concat_axis=0, tiled=True)
        packed = (lax.psum(packed, AXES), jnp.zeros_like(packed))
    else:
        packed, arrived = all_sum_and_route(packed, outgoing, n, n_rows)
    arrived = arrived.reshape(n_rows * CAP, -1)
    upper, basis_stat, basis_rot = factor_and_basis(packed, sketch_stat, arrived)
    return (basis_stat, basis_rot, upper)


def solution(mesh):
    return jax.shard_map(
        per_device,
        mesh=mesh,
        in_specs=(
            P(("grp", "rows"), None),
            P(("grp", "rows"), None),
            P(("grp", "rows"), None),
            P(("grp", "rows")),
            P(),
        ),
        out_specs=(P(("grp", "rows"), None), P(("grp", "rows"), None), P()),
        check_vma=False,
    )
```

```python
import functools

import jax
import jax.numpy as jnp
from jax import lax
from jax.experimental import pallas as pl
from jax.experimental.pallas import tpu as pltpu
from jax.sharding import PartitionSpec as P

CAP = 6
AXES = ("grp", "rows")
HIGHEST = lax.Precision.HIGHEST
GROUP = 8


def sketch_block(block, omega):
    return jnp.dot(block, omega, preferred_element_type=jnp.float32).astype(jnp.bfloat16)


def pack_sym(g):
    h = g.shape[0] // 2
    i = lax.broadcasted_iota(jnp.int32, (h, h), 0)
    j = lax.broadcasted_iota(jnp.int32, (h, h), 1)
    a, b, c = g[:h, :h], g[h:, :h], g[h:, h:]
    m = jnp.where(i >= j, a, c)
    diag_c = jnp.sum(jnp.where(i == j, c, 0.0), axis=0, keepdims=True)
    return jnp.concatenate([b, m, diag_c], axis=0)


def unpack_sym(p):
    h = p.shape[1]
    b, m, diag_c = p[:h], p[h : 2 * h], p[2 * h :]
    i = lax.broadcasted_iota(jnp.int32, (h, h), 0)
    j = lax.broadcasted_iota(jnp.int32, (h, h), 1)
    mt = m.T
    a = jnp.where(i >= j, m, mt)
    c = jnp.where(i < j, m, jnp.where(i > j, mt, diag_c))
    return jnp.concatenate(
        [jnp.concatenate([a, b.T], axis=1), jnp.concatenate([b, c], axis=1)], axis=0
    )


def all_sum_and_route(x, held, n, n_rows):
    bits = n.bit_length() - 1
    row_bits = n_rows.bit_length() - 1
    me = lax.axis_index(AXES)
    width = x.shape[1]
    for b in reversed(range(bits)):
        perm = [(i, i ^ (1 << b)) for i in range(n)]
        if b >= row_bits:
            x = x + lax.ppermute(x, AXES, perm)
            continue
        parts = held.reshape((n_rows >> (b + 1), 2, 1 << b) + held.shape[1:])
        mine = (me >> b) & 1
        keep = jnp.where(mine == 0, parts[:, 0], parts[:, 1])
        away = jnp.where(mine == 0, parts[:, 1], parts[:, 0])
        packet = jnp.concatenate([x, away.astype(jnp.float32).reshape(-1, width)], axis=0)
        got = lax.ppermute(packet, AXES, perm)
        x = x + got[: x.shape[0]]
        came = got[x.shape[0] :].reshape(away.shape).astype(held.dtype)
        lo = jnp.where(mine == 0, keep, came)
        hi = jnp.where(mine == 0, came, keep)
        held = jnp.stack([lo, hi], axis=1).reshape(held.shape)
    return x, held


def _chol_kernel(g_ref, ys_ref, yr_ref, u_ref, bs_ref, br_ref, b_ref, *, panel):
    k = g_ref.shape[1] * 2
    w = 2 * k
    kp = ((k + 127) // 128) * 128
    rows = lax.broadcasted_iota(jnp.int32, (k, k), 0)
    cols = lax.broadcasted_iota(jnp.int32, (k, k), 1)
    h = k // 2
    packed = g_ref[...]
    lower_b, mixed, diag_c = packed[:h], packed[h : 2 * h], packed[2 * h : 2 * h + 1]
    i = lax.broadcasted_iota(jnp.int32, (h, h), 0)
    j = lax.broadcasted_iota(jnp.int32, (h, h), 1)
    mixed_t = mixed.T
    a = jnp.where(i >= j, mixed, mixed_t)
    c = jnp.where(i < j, mixed, jnp.where(i > j, mixed_t, diag_c))
    top = jnp.concatenate([a, lower_b.T], axis=1)
    b_ref[:, :k] = jnp.concatenate([top, jnp.concatenate([lower_b, c], axis=1)], axis=0)
    b_ref[:, k:] = jnp.where(rows == cols, 1.0, 0.0).astype(jnp.float32)
    for p in range(k // panel):
        base = p * panel
        end = base + panel
        pan = b_ref[base:end, :]
        for r in range(0, panel, GROUP):
            piv = base + r
            t0 = (piv // 128) * 128
            top, low = pan[:r], pan[r:]
            m = panel - r
            lane = lax.broadcasted_iota(jnp.int32, (m, 128), 1) + t0
            blk = low[:, t0 : t0 + 128]
            cs = [
                jnp.sum(jnp.where(lane == piv + t, blk, 0.0), axis=1, keepdims=True)
                for t in range(GROUP)
            ]
            coefs, vs = [], []
            for t in range(GROUP):
                c, row = cs[t], low[t : t + 1]
                for u in range(t):
                    lu = coefs[u][t : t + 1]
                    c = c - coefs[u] * lu
                    row = row - lu * vs[u]
                s = lax.rsqrt(c[t : t + 1])
                vs.append(row * s)
                coefs.append(c * s)
            sub = lax.broadcasted_iota(jnp.int32, (m, w), 0)
            upd = low
            for t in range(GROUP):
                upd = upd - coefs[t] * vs[t]
            low = jnp.where(sub >= GROUP, upd, low)
            for t in range(GROUP):
                low = jnp.where(sub == t, vs[t], low)
            pan = jnp.concatenate([top, low], axis=0) if r else low
        sub = lax.broadcasted_iota(jnp.int32, pan.shape, 0) + base
        lane = lax.broadcasted_iota(jnp.int32, pan.shape, 1)
        pan = jnp.where((lane < k) & (lane < sub), 0.0, pan)
        b_ref[base:end, :] = pan
        if end < k:
            part = jnp.where((lane >= end) & (lane < k), pan, 0.0)[:, :kp]
            upd = lax.dot_general(
                part, pan, (((0,), (0,)), ((), ())), precision=HIGHEST,
                preferred_element_type=jnp.float32,
            )
            b_ref[end:, :] = b_ref[end:, :] - upd[end:k]
    u_ref[...] = b_ref[:, :k]
    rest = b_ref[:, k:]
    parts = []
    for _ in range(3):
        term = rest.astype(jnp.bfloat16)
        parts.append(term)
        rest = rest - term.astype(jnp.float32)
    dims = (((1,), (1,)), ((), ()))
    for y_ref, o_ref, flip in ((ys_ref, bs_ref, True), (yr_ref, br_ref, False)):
        if len(y_ref.shape) == 3:
            cap = y_ref.shape[1]
            for s in range(y_ref.shape[0]):
                acc = None
                for part in parts:
                    t = lax.dot_general(y_ref[s], part, dims, preferred_element_type=jnp.float32)
                    acc = t if acc is None else acc + t
                o_ref[s * cap : (s + 1) * cap, :] = acc.astype(o_ref.dtype)
            continue
        n = y_ref.shape[0]
        step = 512 if n % 512 == 0 else n
        for i in range(0, n, step):
            y = y_ref[i : i + step, :]
            acc = None
            for part in parts:
                pair = (part, y) if flip else (y, part)
                t = lax.dot_general(*pair, dims, preferred_element_type=jnp.float32)
                acc = t if acc is None else acc + t
            if flip:
                o_ref[:, i : i + step] = acc.astype(o_ref.dtype)
            else:
                o_ref[i : i + step, :] = acc.astype(o_ref.dtype)


def factor_and_basis(packed, y_stat, y_rot):
    k = packed.shape[1] * 2
    panel = next((p for p in (96, 64, 48, 32, 16, 8) if k % p == 0), None)
    if panel is None:
        lower = jnp.linalg.cholesky(unpack_sym(packed))
        eye = jnp.eye(k, dtype=jnp.float32)
        inverse = lax.linalg.triangular_solve(lower, eye, left_side=True, lower=True)
        basis = [
            jnp.dot(y.astype(jnp.float32), inverse.T, precision=HIGHEST).astype(jnp.bfloat16)
            for y in (y_stat, y_rot.reshape(-1, y_rot.shape[-1]))
        ]
        return lower.T, basis[0], basis[1]
    vmem = pl.BlockSpec(memory_space=pltpu.VMEM)
    upper, basis_stat_t, basis_rot = pl.pallas_call(
        functools.partial(_chol_kernel, panel=panel),
        out_shape=(
            jax.ShapeDtypeStruct((k, k), jnp.float32),
            jax.ShapeDtypeStruct(y_stat.shape[::-1], jnp.bfloat16),
            jax.ShapeDtypeStruct((y_rot.shape[0] * y_rot.shape[1], y_rot.shape[2]), jnp.bfloat16),
        ),
        in_specs=[vmem, vmem, vmem],
        out_specs=(vmem, vmem, vmem),
        scratch_shapes=[pltpu.VMEM((k, 2 * k), jnp.float32)],
    )(packed, y_stat, y_rot)
    return upper, basis_stat_t.T, basis_rot


def per_device(stationary, rotor_rows, owners, counts, omega):
    n_rows = lax.axis_size("rows")
    n_grp = lax.axis_size("grp")
    rot_dev = rotor_rows.shape[0]
    stat_dev = stationary.shape[0]
    total = n_grp * n_rows * (stat_dev + rot_dev)
    k = omega.shape[1]
    targets = owners[:, 0]
    live = lax.iota(jnp.int32, rot_dev) < counts[0]
    onehot = ((targets[:, None] == lax.iota(jnp.int32, n_rows)[None, :]) & live[:, None]).astype(
        jnp.int32
    )
    rank = jnp.sum((jnp.cumsum(onehot, axis=0) - onehot) * onehot, axis=1)
    slot = jnp.where(live, targets * CAP + rank, -1)
    select = (lax.iota(jnp.int32, n_rows * CAP)[:, None] == slot[None, :]).astype(jnp.bfloat16)

    sketch_stat = sketch_block(stationary, omega)
    sketch_rot = sketch_block(rotor_rows, omega)
    rot_live = jnp.where(live[:, None], sketch_rot, jnp.zeros_like(sketch_rot))

    dims = (((0,), (0,)), ((), ()))
    gram = lax.dot_general(sketch_stat, sketch_stat, dims, preferred_element_type=jnp.float32)
    gram = gram + lax.dot_general(rot_live, rot_live, dims, preferred_element_type=jnp.float32)
    gram = gram / total

    outgoing = jnp.dot(select, sketch_rot, preferred_element_type=jnp.float32).astype(jnp.bfloat16)
    outgoing = outgoing.reshape(n_rows, CAP, -1)
    packed = pack_sym(gram)
    n = n_grp * n_rows
    if n & (n - 1) or n_rows & (n_rows - 1) or (CAP * k) % packed.shape[1]:
        arrived = lax.all_to_all(outgoing, "rows", split_axis=0, concat_axis=0, tiled=True)
        packed = lax.psum(packed, AXES)
    else:
        packed, arrived = all_sum_and_route(packed, outgoing, n, n_rows)
    if n_rows > 16:
        arrived = arrived.reshape(1, n_rows * CAP, -1)
    upper, basis_stat, basis_rot = factor_and_basis(packed, sketch_stat, arrived)
    return (basis_stat, basis_rot, upper)


def solution(mesh):
    return jax.shard_map(
        per_device,
        mesh=mesh,
        in_specs=(
            P(("grp", "rows"), None),
            P(("grp", "rows"), None),
            P(("grp", "rows"), None),
            P(("grp", "rows")),
            P(),
        ),
        out_specs=(P(("grp", "rows"), None), P(("grp", "rows"), None), P()),
        check_vma=False,
    )
```

```python
import functools

import jax
import jax.numpy as jnp
from jax import lax
from jax.experimental import pallas as pl
from jax.experimental.pallas import tpu as pltpu
from jax.sharding import PartitionSpec as P

CAP = 6
AXES = ("grp", "rows")
HIGHEST = lax.Precision.HIGHEST
GROUP = 8


def sketch_block(block, omega):
    return jnp.dot(block, omega, preferred_element_type=jnp.float32).astype(jnp.bfloat16)


def pack_sym(g):
    h = g.shape[0] // 2
    i = lax.broadcasted_iota(jnp.int32, (h, h), 0)
    j = lax.broadcasted_iota(jnp.int32, (h, h), 1)
    a, b, c = g[:h, :h], g[h:, :h], g[h:, h:]
    m = jnp.where(i >= j, a, c)
    diag_c = jnp.sum(jnp.where(i == j, c, 0.0), axis=0, keepdims=True)
    return jnp.concatenate([b, m, diag_c], axis=0)


def unpack_sym(p):
    h = p.shape[1]
    b, m, diag_c = p[:h], p[h : 2 * h], p[2 * h :]
    i = lax.broadcasted_iota(jnp.int32, (h, h), 0)
    j = lax.broadcasted_iota(jnp.int32, (h, h), 1)
    mt = m.T
    a = jnp.where(i >= j, m, mt)
    c = jnp.where(i < j, m, jnp.where(i > j, mt, diag_c))
    return jnp.concatenate(
        [jnp.concatenate([a, b.T], axis=1), jnp.concatenate([b, c], axis=1)], axis=0
    )


def all_sum_and_route(x, held, n, n_rows):
    bits = n.bit_length() - 1
    row_bits = n_rows.bit_length() - 1
    me = lax.axis_index(AXES)
    width = x.shape[1]
    for b in reversed(range(bits)):
        perm = [(i, i ^ (1 << b)) for i in range(n)]
        if b >= row_bits:
            x = x + lax.ppermute(x, AXES, perm)
            continue
        parts = held.reshape((n_rows >> (b + 1), 2, 1 << b) + held.shape[1:])
        mine = (me >> b) & 1
        keep = jnp.where(mine == 0, parts[:, 0], parts[:, 1])
        away = jnp.where(mine == 0, parts[:, 1], parts[:, 0])
        packet = jnp.concatenate([x, away.astype(jnp.float32).reshape(-1, width)], axis=0)
        got = lax.ppermute(packet, AXES, perm)
        x = x + got[: x.shape[0]]
        came = got[x.shape[0] :].reshape(away.shape).astype(held.dtype)
        lo = jnp.where(mine == 0, keep, came)
        hi = jnp.where(mine == 0, came, keep)
        held = jnp.stack([lo, hi], axis=1).reshape(held.shape)
    return x, held


def _chol_kernel(g_ref, ys_ref, yr_ref, u_ref, bs_ref, br_ref, b_ref, *, panel):
    k = g_ref.shape[1] * 2
    w = 2 * k
    kp = ((k + 127) // 128) * 128
    rows = lax.broadcasted_iota(jnp.int32, (k, k), 0)
    cols = lax.broadcasted_iota(jnp.int32, (k, k), 1)
    h = k // 2
    packed = g_ref[...]
    lower_b, mixed, diag_c = packed[:h], packed[h : 2 * h], packed[2 * h : 2 * h + 1]
    i = lax.broadcasted_iota(jnp.int32, (h, h), 0)
    j = lax.broadcasted_iota(jnp.int32, (h, h), 1)
    mixed_t = mixed.T
    a = jnp.where(i >= j, mixed, mixed_t)
    c = jnp.where(i < j, mixed, jnp.where(i > j, mixed_t, diag_c))
    top = jnp.concatenate([a, lower_b.T], axis=1)
    b_ref[:, :k] = jnp.concatenate([top, jnp.concatenate([lower_b, c], axis=1)], axis=0)
    b_ref[:, k:] = jnp.where(rows == cols, 1.0, 0.0).astype(jnp.float32)
    for p in range(k // panel):
        base = p * panel
        end = base + panel
        pan = b_ref[base:end, :]
        for r in range(0, panel, GROUP):
            piv = base + r
            t0 = (piv // 128) * 128
            top, low = pan[:r], pan[r:]
            m = panel - r
            lane = lax.broadcasted_iota(jnp.int32, (m, 128), 1) + t0
            blk = low[:, t0 : t0 + 128]
            cs = [
                jnp.sum(jnp.where(lane == piv + t, blk, 0.0), axis=1, keepdims=True)
                for t in range(GROUP)
            ]
            coefs, vs = [], []
            for t in range(GROUP):
                c, row = cs[t], low[t : t + 1]
                for u in range(t):
                    lu = coefs[u][t : t + 1]
                    c = c - coefs[u] * lu
                    row = row - lu * vs[u]
                s = lax.rsqrt(c[t : t + 1])
                vs.append(row * s)
                coefs.append(c * s)
            sub = lax.broadcasted_iota(jnp.int32, (m, w), 0)
            upd = low
            for t in range(GROUP):
                upd = upd - coefs[t] * vs[t]
            low = jnp.where(sub >= GROUP, upd, low)
            for t in range(GROUP):
                low = jnp.where(sub == t, vs[t], low)
            pan = jnp.concatenate([top, low], axis=0) if r else low
        sub = lax.broadcasted_iota(jnp.int32, pan.shape, 0) + base
        lane = lax.broadcasted_iota(jnp.int32, pan.shape, 1)
        pan = jnp.where((lane < k) & (lane < sub), 0.0, pan)
        b_ref[base:end, :] = pan
        if end < k:
            part = jnp.where((lane >= end) & (lane < k), pan, 0.0)[:, :kp]
            upd = lax.dot_general(
                part, pan, (((0,), (0,)), ((), ())), precision=lax.Precision.HIGH,
                preferred_element_type=jnp.float32,
            )
            b_ref[end:, :] = b_ref[end:, :] - upd[end:k]
    u_ref[...] = b_ref[:, :k]
    rest = b_ref[:, k:]
    parts = []
    for _ in range(3):
        term = rest.astype(jnp.bfloat16)
        parts.append(term)
        rest = rest - term.astype(jnp.float32)
    dims = (((1,), (1,)), ((), ()))
    for y_ref, o_ref, flip in ((ys_ref, bs_ref, True), (yr_ref, br_ref, False)):
        n = y_ref.shape[0]
        step = 512 if n % 512 == 0 else n
        for i in range(0, n, step):
            y = y_ref[i : i + step, :]
            acc = None
            for part in parts:
                pair = (part, y) if flip else (y, part)
                t = lax.dot_general(*pair, dims, preferred_element_type=jnp.float32)
                acc = t if acc is None else acc + t
            if flip:
                o_ref[:, i : i + step] = acc.astype(o_ref.dtype)
            else:
                o_ref[i : i + step, :] = acc.astype(o_ref.dtype)


def factor_and_basis(packed, y_stat, y_rot):
    k = packed.shape[1] * 2
    panel = next((p for p in (96, 64, 48, 32, 16, 8) if k % p == 0), None)
    if panel is None:
        lower = jnp.linalg.cholesky(unpack_sym(packed))
        eye = jnp.eye(k, dtype=jnp.float32)
        inverse = lax.linalg.triangular_solve(lower, eye, left_side=True, lower=True)
        basis = [
            jnp.dot(y.astype(jnp.float32), inverse.T, precision=HIGHEST).astype(jnp.bfloat16)
            for y in (y_stat, y_rot)
        ]
        return lower.T, basis[0], basis[1]
    vmem = pl.BlockSpec(memory_space=pltpu.VMEM)
    upper, basis_stat_t, basis_rot = pl.pallas_call(
        functools.partial(_chol_kernel, panel=panel),
        out_shape=(
            jax.ShapeDtypeStruct((k, k), jnp.float32),
            jax.ShapeDtypeStruct(y_stat.shape[::-1], jnp.bfloat16),
            jax.ShapeDtypeStruct(y_rot.shape, jnp.bfloat16),
        ),
        in_specs=[vmem, vmem, vmem],
        out_specs=(vmem, vmem, vmem),
        scratch_shapes=[pltpu.VMEM((k, 2 * k), jnp.float32)],
    )(packed, y_stat, y_rot)
    return upper, basis_stat_t.T, basis_rot


def per_device(stationary, rotor_rows, owners, counts, omega):
    n_rows = lax.axis_size("rows")
    n_grp = lax.axis_size("grp")
    rot_dev = rotor_rows.shape[0]
    stat_dev = stationary.shape[0]
    total = n_grp * n_rows * (stat_dev + rot_dev)
    k = omega.shape[1]
    targets = owners[:, 0]
    live = lax.iota(jnp.int32, rot_dev) < counts[0]
    onehot = ((targets[:, None] == lax.iota(jnp.int32, n_rows)[None, :]) & live[:, None]).astype(
        jnp.int32
    )
    rank = jnp.sum((jnp.cumsum(onehot, axis=0) - onehot) * onehot, axis=1)
    slot = jnp.where(live, targets * CAP + rank, -1)
    select = (lax.iota(jnp.int32, n_rows * CAP)[:, None] == slot[None, :]).astype(jnp.bfloat16)

    sketch_stat = sketch_block(stationary, omega)
    sketch_rot = sketch_block(rotor_rows, omega)
    rot_live = jnp.where(live[:, None], sketch_rot, jnp.zeros_like(sketch_rot))

    dims = (((0,), (0,)), ((), ()))
    gram = lax.dot_general(sketch_stat, sketch_stat, dims, preferred_element_type=jnp.float32)
    gram = gram + lax.dot_general(rot_live, rot_live, dims, preferred_element_type=jnp.float32)
    gram = gram / total

    outgoing = jnp.dot(select, sketch_rot, preferred_element_type=jnp.float32).astype(jnp.bfloat16)
    outgoing = outgoing.reshape(n_rows, CAP, -1)
    packed = pack_sym(gram)
    n = n_grp * n_rows
    if n & (n - 1) or n_rows & (n_rows - 1) or (CAP * k) % packed.shape[1]:
        arrived = lax.all_to_all(outgoing, "rows", split_axis=0, concat_axis=0, tiled=True)
        packed = lax.psum(packed, AXES)
    else:
        packed, arrived = all_sum_and_route(packed, outgoing, n, n_rows)
    arrived = arrived.reshape(n_rows * CAP, -1)
    upper, basis_stat, basis_rot = factor_and_basis(packed, sketch_stat, arrived)
    return (basis_stat, basis_rot, upper)


def solution(mesh):
    return jax.shard_map(
        per_device,
        mesh=mesh,
        in_specs=(
            P(("grp", "rows"), None),
            P(("grp", "rows"), None),
            P(("grp", "rows"), None),
            P(("grp", "rows")),
            P(),
        ),
        out_specs=(P(("grp", "rows"), None), P(("grp", "rows"), None), P()),
        check_vma=False,
    )
```
